128 devices in a mesh: pool: 4 (over x_hi, core), grp: 4 (over y), tp: 8 (over z, x_lo).
Axes of the slice: x: 4 (x_hi: 2, x_lo: 2; x = x_hi * 2 + x_lo), y: 4, z: 4, core: 2. Of those that a mesh axis runs over, the one named last changes fastest.
Arguments:
- hidden: bfloat16 [1024, 8192], P('pool', 'grp'), may hold values from -6 to 6
- attn_gain: float32 [8192], P('grp'), may hold values from 0.25 to 1.75
- w_query: bfloat16 [8192, 8192], P('grp', 'tp'), may hold values from -0.0625 to 0.0625
- w_key: bfloat16 [8192, 1024], P('grp', 'tp'), may hold values from -1 to 1
- w_value: bfloat16 [8192, 1024], P('grp', 'tp'), may hold values from -0.0625 to 0.0625
- w_out: bfloat16 [8192, 8192], P('tp', 'grp'), may hold values from -0.0625 to 0.0625
- prefix_keys: bfloat16 [8, 16384, 1024], P('pool', 'grp', 'tp'), may hold values from -300 to 300
- prefix_values: bfloat16 [8, 16384, 1024], P('pool', 'grp', 'tp'), may hold values from -6 to 6
- suffix_keys: bfloat16 [1024, 256, 1024], P('pool', 'grp', 'tp'), may hold values from -300 to 300
- suffix_values: bfloat16 [1024, 256, 1024], P('pool', 'grp', 'tp'), may hold values from -6 to 6
- prefix_ids: int32 [1024], P('pool'), may hold values from 0 to 7, as said below
- suffix_lens: int32 [1024], P('pool'), may hold values from 1 to 256, as said below
- ffn_gain: float32 [8192], P('grp'), may hold values from 0.25 to 1.75
- w_gate: bfloat16 [8192, 14336], P('grp', ('pool', 'tp')), may hold values from -0.0625 to 0.0625
- w_up: bfloat16 [8192, 14336], P('grp', ('pool', 'tp')), may hold values from -0.0625 to 0.0625
- w_down: bfloat16 [14336, 8192], P(('pool', 'tp'), 'grp'), may hold values from -0.046875 to 0.046875
Outputs:
- result: bfloat16 [1024, 8192], P(('pool', 'tp'), 'grp')
The draws below stay inside these ranges and needn't reach their ends.
Inputs may be any that keep to these rules, and one draw needn't show every extreme that they name: `prefix_ids`: within rows p * 256 to (p + 1) * 256 - 1, each of the prefixes p * 2 to (p + 1) * 2 - 1 is named by exactly 128 streams, and no other prefix is named. `suffix_lens`: each block of 256 streams holds a stream of length 256 and one of length 1.
All inputs are finite; a program needn't handle non-finite values.
Results may differ from the reference program's by a relative error of at most 0.015.
Values may be sent and summed in bfloat16 or wider, within the bound.
No kernel may reach another device: no remote copies, remote signals or barrier semaphores. Data moves between devices by JAX's collectives and lax.ppermute only.
A program may use at most 192 MiB of HBM per device.

```python
import math
import jax
import jax.numpy as jnp
from jax import lax

D = 8192
QH = 64
KVH = 8
HD = 128
F = 14336
S_POOL = 256
L_PRE = 16384
L_SUF = 256
P_LOC = 2
STREAMS = 1024
PREFIXES = 8


def draw_hidden(key, part):
    column = jnp.arange(D, dtype=jnp.float32) / max(D - 1, 1)
    base_key = jax.random.fold_in(key, 505)
    baseline = jax.random.truncated_normal(base_key, -4.0, 4.0, (STREAMS, D), jnp.float32)
    scales = 0.3 * jnp.exp(column * math.log(5.0))
    return (baseline * scales[None, :]).astype(jnp.bfloat16)


def planted_keys(key, row_count, length, pair_count):
    width = KVH * HD
    base_key, place_key, strength_key, sink_key = jax.random.split(key, 4)
    baseline = jax.random.truncated_normal(base_key, -6.0, 6.0, (row_count, length, width), jnp.float32)
    lowest = 8.0
    highest = 64.0
    places = jax.random.randint(place_key, (row_count, pair_count), 0, length - 1, dtype=jnp.int32)
    strength = jnp.exp(jax.random.uniform(strength_key, (row_count, pair_count), jnp.float32, math.log(lowest), math.log(highest)))
    sink_rows = jax.random.truncated_normal(sink_key, -3.0, 3.0, (row_count, pair_count, width), jnp.float32)
    slot_range = jnp.arange(length, dtype=jnp.int32)
    planted = baseline
    for pair_number in range(pair_count):
        vector = (strength[:, pair_number, None] * sink_rows[:, pair_number, :])[:, None, :]
        first_hit = (slot_range[None, :] == places[:, pair_number, None])[:, :, None]
        second_hit = (slot_range[None, :] == places[:, pair_number, None] + 1)[:, :, None]
        planted = jnp.where(first_hit, vector, planted)
        planted = jnp.where(second_hit, vector * 1.012, planted)
    return planted.astype(jnp.bfloat16)


def draw_prefix_keys(key, part):
    return planted_keys(jax.random.fold_in(key, 101), PREFIXES, L_PRE, 3)


def draw_suffix_keys(key, part):
    return planted_keys(jax.random.fold_in(key, 202), STREAMS, L_SUF, 2)


def shuffle_block(block_key):
    return jax.random.permutation(block_key, S_POOL).astype(jnp.int32)


def draw_prefix_ids(key, part):
    blocks = STREAMS // S_POOL
    per_group = S_POOL // P_LOC
    block_keys = jax.random.split(jax.random.fold_in(key, 303), blocks)
    shuffled = jax.vmap(shuffle_block)(block_keys)
    slices = jnp.arange(blocks, dtype=jnp.int32)[:, None]
    return (slices * P_LOC + shuffled // per_group).reshape(STREAMS).astype(jnp.int32)


def draw_suffix_lens(key, part):
    offset = jnp.arange(STREAMS, dtype=jnp.int32) % S_POOL
    lengths = jax.random.randint(jax.random.fold_in(key, 404), (STREAMS,), 1, L_SUF + 1, dtype=jnp.int32)
    return jnp.where(offset == 0, L_SUF, jnp.where(offset == 1, 1, lengths))


def steps_of(rng, shape, shards, low, top_value):
    def one(position, parts):
        steps = jax.random.uniform(jax.random.fold_in(jax.random.fold_in(rng, 6), position), (parts,), jnp.float32, low / len(shards), top_value / len(shards))
        return jnp.repeat(jnp.exp(steps), shape[position] // parts).reshape((-1,) + (1,) * (len(shape) - position - 1))

    level = one(*shards[0])
    for cut in shards[1:]:
        level = level * one(*cut)
    return level


def bell_draw(own_key, dims, scale, most, cuts=(), held_as=jnp.bfloat16):
    values = scale * jax.random.normal(own_key, dims, jnp.float32)
    if cuts:
        values = values * steps_of(own_key, dims, cuts, -0.22, 0.18)
    return jnp.clip(values, -most, most).astype(held_as)


def setup_inputs(seed: int = 0) -> dict:
    splits = jax.random.split(jax.random.key(seed), 17)
    hidden = draw_hidden(jax.random.fold_in(splits[16], 71), 0)
    attn_gain = jnp.clip(1.0 + 0.15 * jax.random.normal(splits[1], (D,), jnp.float32), 0.25, 1.75)
    w_query = bell_draw(splits[2], (D, QH * HD), D ** -0.5, 0.0625, ((0, 4), (1, 8)))
    w_key = bell_draw(splits[3], (D, KVH * HD), (max(D // 256, 1)) ** -0.5, 1.0, ((0, 4), (1, 8)))
    w_value = bell_draw(splits[4], (D, KVH * HD), D ** -0.5, 0.0625, ((0, 4), (1, 8)))
    w_out = bell_draw(splits[5], (QH * HD, D), (QH * HD) ** -0.5, 0.0625, ((0, 8), (1, 4)))
    prefix_keys = draw_prefix_keys(jax.random.fold_in(splits[16], 71), 0)
    prefix_values = bell_draw(splits[7], (PREFIXES, L_PRE, KVH * HD), 1.0, 6.0, ((0, 4), (1, 4), (2, 8)))
    suffix_keys = draw_suffix_keys(jax.random.fold_in(splits[16], 71), 0)
    suffix_values = bell_draw(splits[9], (STREAMS, L_SUF, KVH * HD), 1.0, 6.0, ((0, 4), (1, 4), (2, 8)))
    prefix_ids = draw_prefix_ids(jax.random.fold_in(splits[16], 71), 0)
    suffix_lens = draw_suffix_lens(jax.random.fold_in(splits[16], 71), 0)
    ffn_gain = jnp.clip(1.0 + 0.15 * jax.random.normal(splits[12], (D,), jnp.float32), 0.25, 1.75)
    w_gate = bell_draw(splits[13], (D, F), D ** -0.5, 0.0625, ((0, 4), (1, 32)))
    w_up = bell_draw(splits[14], (D, F), D ** -0.5, 0.0625, ((0, 4), (1, 32)))
    w_down = bell_draw(splits[15], (F, D), F ** -0.5, 0.046875, ((0, 32), (1, 4)))
    return {"hidden": hidden, "attn_gain": attn_gain, "w_query": w_query, "w_key": w_key, "w_value": w_value, "w_out": w_out, "prefix_keys": prefix_keys, "prefix_values": prefix_values, "suffix_keys": suffix_keys, "suffix_values": suffix_values, "prefix_ids": prefix_ids, "suffix_lens": suffix_lens, "ffn_gain": ffn_gain, "w_gate": w_gate, "w_up": w_up, "w_down": w_down}


epsilon = 1e-05

def rms_normed(values, gain):
    inverse = lax.rsqrt(lax.optimization_barrier(jnp.mean(values * values, axis=1, keepdims=True)) + epsilon)
    return (values * inverse * gain).astype(jnp.bfloat16)

def reference(hidden, attn_gain, w_query, w_key, w_value, w_out, prefix_keys, prefix_values, suffix_keys, suffix_values, prefix_ids, suffix_lens, ffn_gain, w_gate, w_up, w_down):
    hidden_float = hidden.astype(jnp.float32)
    normed = rms_normed(hidden_float, attn_gain)
    query = jnp.dot(normed, w_query, preferred_element_type=jnp.float32).astype(jnp.bfloat16)
    key_new = jnp.dot(normed, w_key, preferred_element_type=jnp.float32).astype(jnp.bfloat16)
    value_new = jnp.dot(normed, w_value, preferred_element_type=jnp.float32).astype(jnp.bfloat16)
    groups = QH // KVH
    factor = 1.0 / math.sqrt(HD)

    def one_stream(items):
        query_row, key_row, value_row, prefix_at, length, suffix_key, suffix_value = items
        pre_key = lax.dynamic_index_in_dim(prefix_keys, prefix_at.astype(jnp.int32), 0, keepdims=False)
        pre_value = lax.dynamic_index_in_dim(prefix_values, prefix_at.astype(jnp.int32), 0, keepdims=False)
        heads = query_row.astype(jnp.float32).reshape(KVH, groups, HD)
        pre_scores = jnp.einsum('kgd,jkd->kgj', heads, pre_key.astype(jnp.float32).reshape(L_PRE, KVH, HD)) * factor
        suf_scores = jnp.einsum('kgd,jkd->kgj', heads, suffix_key.astype(jnp.float32).reshape(L_SUF, KVH, HD)) * factor
        valid = jnp.arange(L_SUF, dtype=jnp.int32) < length
        suf_scores = jnp.where(valid[None, None, :], suf_scores, -1e+30)
        own_score = jnp.einsum('kgd,kd->kg', heads, key_row.astype(jnp.float32).reshape(KVH, HD)) * factor
        peak = jnp.maximum(jnp.maximum(pre_scores.max(axis=2), suf_scores.max(axis=2)), own_score)
        pre_weights = jnp.exp(pre_scores - peak[:, :, None]).astype(jnp.bfloat16).astype(jnp.float32)
        suf_weights = jnp.where(valid[None, None, :], jnp.exp(suf_scores - peak[:, :, None]), 0.0).astype(jnp.bfloat16).astype(jnp.float32)
        own_weight = jnp.exp(own_score - peak).astype(jnp.bfloat16).astype(jnp.float32)
        total = pre_weights.sum(axis=2) + suf_weights.sum(axis=2) + own_weight
        numer = jnp.einsum('kgj,jkd->kgd', pre_weights, pre_value.astype(jnp.float32).reshape(L_PRE, KVH, HD))
        numer = numer + jnp.einsum('kgj,jkd->kgd', suf_weights, suffix_value.astype(jnp.float32).reshape(L_SUF, KVH, HD))
        numer = numer + own_weight[:, :, None] * value_row.astype(jnp.float32).reshape(KVH, 1, HD)
        return (numer / total[:, :, None]).reshape(QH * HD).astype(jnp.bfloat16)
    attended = lax.map(one_stream, (query, key_new, value_new, prefix_ids, suffix_lens, suffix_keys, suffix_values))
    middle = (hidden_float + jnp.dot(attended, w_out, preferred_element_type=jnp.float32)).astype(jnp.bfloat16)
    middle_float = middle.astype(jnp.float32)
    normed_ffn = rms_normed(middle_float, ffn_gain)
    gate = jnp.dot(normed_ffn, w_gate, preferred_element_type=jnp.float32)
    upward = jnp.dot(normed_ffn, w_up, preferred_element_type=jnp.float32)
    act = (jax.nn.silu(gate) * upward).astype(jnp.bfloat16)
    return (middle_float + jnp.dot(act, w_down, preferred_element_type=jnp.float32)).astype(jnp.bfloat16)
```

```python
import math

import jax
import jax.numpy as jnp
from jax import lax
from jax.sharding import PartitionSpec as P

D = 8192
HD = 128


epsilon = 1e-05


def joined(array, axis, combine):
    everything = jax.tree.map(lambda part: lax.all_gather(part, axis), array)
    first = jax.tree.map(lambda part: part[0], everything)

    def lap(k, so_far):
        return combine(so_far, jax.tree.map(lambda part: part[k], everything))

    return lax.fori_loop(1, lax.axis_size(axis), lap, first)


def combine_parts(earlier, later):
    peak_one, total_one, numer_one = earlier
    peak_two, total_two, numer_two = later
    peak = jnp.maximum(peak_one, peak_two)
    scale_one = jnp.exp(peak_one - peak)
    scale_two = jnp.exp(peak_two - peak)
    total = total_one * scale_one + total_two * scale_two
    numer = numer_one * scale_one[..., None] + numer_two * scale_two[..., None]
    return (peak, total, numer)


def body(
    hidden,
    attn_gain,
    w_query,
    w_key,
    w_value,
    w_out,
    prefix_keys,
    prefix_values,
    suffix_keys,
    suffix_values,
    prefix_ids,
    suffix_lens,
    ffn_gain,
    w_gate,
    w_up,
    w_down,
):
    stream_count = hidden.shape[0]
    hidden_float = hidden.astype(jnp.float32)
    squares = lax.psum(jnp.sum(hidden_float * hidden_float, axis=1), "grp")
    inverse = lax.rsqrt(squares / D + epsilon)
    normed = (hidden_float * inverse[:, None] * attn_gain).astype(jnp.bfloat16)
    part_query = jnp.dot(normed, w_query, preferred_element_type=jnp.float32)
    part_key = jnp.dot(normed, w_key, preferred_element_type=jnp.float32)
    part_value = jnp.dot(normed, w_value, preferred_element_type=jnp.float32)
    query, key_new, value_new = lax.psum((part_query, part_key, part_value), "grp")
    query = query.astype(jnp.bfloat16)
    key_new = key_new.astype(jnp.bfloat16)
    value_new = value_new.astype(jnp.bfloat16)
    kv_local = w_key.shape[1] // HD
    q_local = w_query.shape[1] // HD
    groups = q_local // kv_local
    prefix_local = prefix_keys.shape[0]
    pre_length = prefix_keys.shape[1]
    suf_length = suffix_keys.shape[1]
    factor = 1.0 / math.sqrt(HD)
    heads = query.reshape(stream_count, kv_local, groups, HD)
    pre_key = prefix_keys.reshape(prefix_local, pre_length, kv_local, HD)
    pre_value = prefix_values.reshape(prefix_local, pre_length, kv_local, HD)
    suf_key = suffix_keys.reshape(stream_count, suf_length, kv_local, HD)
    suf_value = suffix_values.reshape(stream_count, suf_length, kv_local, HD)
    local_prefix = prefix_ids - lax.axis_index("pool") * prefix_local
    per_group = stream_count // prefix_local
    one_hot = (local_prefix[:, None] == jnp.arange(prefix_local, dtype=jnp.int32)[None, :]).astype(
        jnp.int32
    )
    rank_within = jnp.sum(jnp.cumsum(one_hot, axis=0) * one_hot, axis=1) - 1
    target = local_prefix * per_group + rank_within
    group_order = (
        jnp.zeros((stream_count,), jnp.int32)
        .at[target]
        .set(jnp.arange(stream_count, dtype=jnp.int32))
    )
    grouped = heads[group_order].reshape(prefix_local, per_group, kv_local, groups, HD)
    pre_scores = (
        jnp.einsum("pskgd,pjkd->pskgj", grouped, pre_key, preferred_element_type=jnp.float32)
        * factor
    )
    pre_peak = pre_scores.max(axis=4).reshape(stream_count, kv_local, groups)[target]
    positions = lax.axis_index("grp") * suf_length + jnp.arange(suf_length, dtype=jnp.int32)
    valid = (positions[None, :] < suffix_lens[:, None])[:, None, None, :]
    suf_scores = (
        jnp.einsum("skgd,sjkd->skgj", heads, suf_key, preferred_element_type=jnp.float32) * factor
    )
    suf_scores = jnp.where(valid, suf_scores, -1e30)
    peak = jnp.maximum(pre_peak, suf_scores.max(axis=3))
    peak_grouped = peak[group_order].reshape(prefix_local, per_group, kv_local, groups)
    pre_weights = jnp.exp(pre_scores - peak_grouped[..., None]).astype(jnp.bfloat16)
    pre_total = (
        pre_weights.astype(jnp.float32).sum(axis=4).reshape(stream_count, kv_local, groups)[target]
    )
    pre_numer = jnp.einsum(
        "pskgj,pjkd->pskgd", pre_weights, pre_value, preferred_element_type=jnp.float32
    )
    pre_numer = pre_numer.reshape(stream_count, kv_local, groups, HD)[target]
    suf_weights = jnp.where(valid, jnp.exp(suf_scores - peak[:, :, :, None]), 0.0).astype(
        jnp.bfloat16
    )
    total = pre_total + suf_weights.astype(jnp.float32).sum(axis=3)
    numer = pre_numer + jnp.einsum(
        "skgj,sjkd->skgd", suf_weights, suf_value, preferred_element_type=jnp.float32
    )
    flat = stream_count, kv_local * groups
    packed = jnp.concatenate(
        [numer.reshape(stream_count, -1), peak.reshape(flat), total.reshape(flat)], axis=1
    )
    everything = lax.all_gather(packed, "grp")
    width = kv_local * groups * HD
    heads_local = kv_local * groups
    all_numer = everything[:, :, :width].reshape(-1, stream_count, kv_local, groups, HD)
    all_peak = everything[:, :, width : width + heads_local].reshape(
        -1, stream_count, kv_local, groups
    )
    all_total = everything[:, :, width + heads_local :].reshape(-1, stream_count, kv_local, groups)
    peak = all_peak.max(axis=0)
    scales = jnp.exp(all_peak - peak[None])
    total = jnp.sum(all_total * scales, axis=0)
    numer = jnp.sum(all_numer * scales[..., None], axis=0)
    own_score = (
        jnp.einsum(
            "skgd,skd->skg",
            heads,
            key_new.reshape(stream_count, kv_local, HD),
            preferred_element_type=jnp.float32,
        )
        * factor
    )
    new_peak = jnp.maximum(peak, own_score)
    rescale = jnp.exp(peak - new_peak)
    own_weight = jnp.exp(own_score - new_peak).astype(jnp.bfloat16).astype(jnp.float32)
    total = total * rescale + own_weight
    own_value = value_new.reshape(stream_count, kv_local, 1, HD).astype(jnp.float32)
    numer = numer * rescale[..., None] + own_weight[..., None] * own_value
    attended = (numer / total[..., None]).reshape(stream_count, q_local * HD).astype(jnp.bfloat16)
    partial_out = jnp.dot(attended, w_out, preferred_element_type=jnp.float32)
    share = stream_count // lax.axis_size("tp")
    tp_start = lax.axis_index("tp") * share
    summed = lax.psum_scatter(
        partial_out.astype(jnp.bfloat16), "tp", scatter_dimension=0, tiled=True
    )
    own_hidden = lax.dynamic_slice_in_dim(hidden_float, tp_start, share, 0)
    middle = (own_hidden + summed.astype(jnp.float32)).astype(jnp.bfloat16)
    middle_float = middle.astype(jnp.float32)
    ffn_squares = lax.psum(jnp.sum(middle_float * middle_float, axis=1), "grp")
    ffn_inverse = lax.rsqrt(ffn_squares / D + epsilon)
    normed_own = (middle_float * ffn_inverse[:, None] * ffn_gain).astype(jnp.bfloat16)
    normed_ffn = lax.all_gather(normed_own, ("pool", "tp"), axis=0, tiled=True)
    hidden_units = w_gate.shape[1]
    part_gate = jnp.dot(normed_ffn, w_gate, preferred_element_type=jnp.float32)
    part_upward = jnp.dot(normed_ffn, w_up, preferred_element_type=jnp.float32)
    both = jnp.concatenate([part_gate, part_upward], axis=1).astype(jnp.bfloat16)
    reduced = lax.psum_scatter(both, "grp", scatter_dimension=0, tiled=True).astype(jnp.float32)
    gate = reduced[:, :hidden_units]
    upward = reduced[:, hidden_units:]
    act = (jax.nn.silu(gate) * upward).astype(jnp.bfloat16)
    act_all = lax.all_gather(act, "grp", axis=0, tiled=True)
    down = jnp.dot(act_all, w_down, preferred_element_type=jnp.float32)
    returned = lax.psum_scatter(
        down.astype(jnp.bfloat16), ("pool", "tp"), scatter_dimension=0, tiled=True
    )
    return (middle_float + returned.astype(jnp.float32)).astype(jnp.bfloat16)


def solution(mesh):
    return jax.shard_map(
        body,
        mesh=mesh,
        in_specs=(
            P("pool", "grp"),
            P("grp"),
            P("grp", "tp"),
            P("grp", "tp"),
            P("grp", "tp"),
            P("tp", "grp"),
            P("pool", "grp", "tp"),
            P("pool", "grp", "tp"),
            P("pool", "grp", "tp"),
            P("pool", "grp", "tp"),
            P("pool"),
            P("pool"),
            P("grp"),
            P("grp", ("pool", "tp")),
            P("grp", ("pool", "tp")),
            P(("pool", "tp"), "grp"),
        ),
        out_specs=P(("pool", "tp"), "grp"),
        check_vma=False,
    )
```

```python
import math

import jax
import jax.numpy as jnp
from jax import lax
from jax.sharding import PartitionSpec as P

D = 8192
HD = 128


epsilon = 1e-05


def joined(array, axis, combine):
    everything = jax.tree.map(lambda part: lax.all_gather(part, axis), array)
    first = jax.tree.map(lambda part: part[0], everything)

    def lap(k, so_far):
        return combine(so_far, jax.tree.map(lambda part: part[k], everything))

    return lax.fori_loop(1, lax.axis_size(axis), lap, first)


def combine_parts(earlier, later):
    peak_one, total_one, numer_one = earlier
    peak_two, total_two, numer_two = later
    peak = jnp.maximum(peak_one, peak_two)
    scale_one = jnp.exp(peak_one - peak)
    scale_two = jnp.exp(peak_two - peak)
    total = total_one * scale_one + total_two * scale_two
    numer = numer_one * scale_one[..., None] + numer_two * scale_two[..., None]
    return (peak, total, numer)


def body(
    hidden,
    attn_gain,
    w_query,
    w_key,
    w_value,
    w_out,
    prefix_keys,
    prefix_values,
    suffix_keys,
    suffix_values,
    prefix_ids,
    suffix_lens,
    ffn_gain,
    w_gate,
    w_up,
    w_down,
):
    stream_count = hidden.shape[0]
    hidden_float = hidden.astype(jnp.float32)
    squares = lax.psum(jnp.sum(hidden_float * hidden_float, axis=1), "grp")
    inverse = lax.rsqrt(squares / D + epsilon)
    normed = (hidden_float * inverse[:, None] * attn_gain).astype(jnp.bfloat16)
    part_query = jnp.dot(normed, w_query, preferred_element_type=jnp.float32)
    part_key = jnp.dot(normed, w_key, preferred_element_type=jnp.float32)
    part_value = jnp.dot(normed, w_value, preferred_element_type=jnp.float32)
    query, key_new, value_new = lax.psum((part_query, part_key, part_value), "grp")
    query = query.astype(jnp.bfloat16)
    key_new = key_new.astype(jnp.bfloat16)
    value_new = value_new.astype(jnp.bfloat16)
    kv_local = w_key.shape[1] // HD
    q_local = w_query.shape[1] // HD
    groups = q_local // kv_local
    prefix_local = prefix_keys.shape[0]
    pre_length = prefix_keys.shape[1]
    suf_length = suffix_keys.shape[1]
    factor = 1.0 / math.sqrt(HD)
    heads = query.reshape(stream_count, kv_local, groups, HD)
    pre_key = prefix_keys.reshape(prefix_local, pre_length, kv_local, HD)
    pre_value = prefix_values.reshape(prefix_local, pre_length, kv_local, HD)
    suf_key = suffix_keys.reshape(stream_count, suf_length, kv_local, HD)
    suf_value = suffix_values.reshape(stream_count, suf_length, kv_local, HD)
    pool_index = lax.axis_index("hi") * lax.axis_size("core") + lax.axis_index("core")
    local_prefix = prefix_ids - pool_index * prefix_local
    per_group = stream_count // prefix_local
    one_hot = (local_prefix[:, None] == jnp.arange(prefix_local, dtype=jnp.int32)[None, :]).astype(
        jnp.int32
    )
    rank_within = jnp.sum(jnp.cumsum(one_hot, axis=0) * one_hot, axis=1) - 1
    target = local_prefix * per_group + rank_within
    group_order = (
        jnp.zeros((stream_count,), jnp.int32)
        .at[target]
        .set(jnp.arange(stream_count, dtype=jnp.int32))
    )
    grouped = heads[group_order].reshape(prefix_local, per_group, kv_local, groups, HD)
    pre_scores = (
        jnp.einsum("pskgd,pjkd->pskgj", grouped, pre_key, preferred_element_type=jnp.float32)
        * factor
    )
    pre_peak = pre_scores.max(axis=4).reshape(stream_count, kv_local, groups)[target]
    positions = lax.axis_index("grp") * suf_length + jnp.arange(suf_length, dtype=jnp.int32)
    valid = (positions[None, :] < suffix_lens[:, None])[:, None, None, :]
    suf_scores = (
        jnp.einsum("skgd,sjkd->skgj", heads, suf_key, preferred_element_type=jnp.float32) * factor
    )
    suf_scores = jnp.where(valid, suf_scores, -1e30)
    peak = jnp.maximum(pre_peak, suf_scores.max(axis=3))
    peak_grouped = peak[group_order].reshape(prefix_local, per_group, kv_local, groups)
    pre_weights = jnp.exp(pre_scores - peak_grouped[..., None]).astype(jnp.bfloat16)
    pre_total = (
        pre_weights.astype(jnp.float32).sum(axis=4).reshape(stream_count, kv_local, groups)[target]
    )
    pre_numer = jnp.einsum(
        "pskgj,pjkd->pskgd", pre_weights, pre_value, preferred_element_type=jnp.float32
    )
    pre_numer = pre_numer.reshape(stream_count, kv_local, groups, HD)[target]
    suf_weights = jnp.where(valid, jnp.exp(suf_scores - peak[:, :, :, None]), 0.0).astype(
        jnp.bfloat16
    )
    total = pre_total + suf_weights.astype(jnp.float32).sum(axis=3)
    numer = pre_numer + jnp.einsum(
        "skgj,sjkd->skgd", suf_weights, suf_value, preferred_element_type=jnp.float32
    )
    flat = stream_count, kv_local * groups
    packed = jnp.concatenate(
        [numer.reshape(stream_count, -1), peak.reshape(flat), total.reshape(flat)], axis=1
    )
    everything = lax.all_gather(packed, "grp")
    width = kv_local * groups * HD
    heads_local = kv_local * groups
    all_numer = everything[:, :, :width].reshape(-1, stream_count, kv_local, groups, HD)
    all_peak = everything[:, :, width : width + heads_local].reshape(
        -1, stream_count, kv_local, groups
    )
    all_total = everything[:, :, width + heads_local :].reshape(-1, stream_count, kv_local, groups)
    peak = all_peak.max(axis=0)
    scales = jnp.exp(all_peak - peak[None])
    total = jnp.sum(all_total * scales, axis=0)
    numer = jnp.sum(all_numer * scales[..., None], axis=0)
    own_score = (
        jnp.einsum(
            "skgd,skd->skg",
            heads,
            key_new.reshape(stream_count, kv_local, HD),
            preferred_element_type=jnp.float32,
        )
        * factor
    )
    new_peak = jnp.maximum(peak, own_score)
    rescale = jnp.exp(peak - new_peak)
    own_weight = jnp.exp(own_score - new_peak).astype(jnp.bfloat16).astype(jnp.float32)
    total = total * rescale + own_weight
    own_value = value_new.reshape(stream_count, kv_local, 1, HD).astype(jnp.float32)
    numer = numer * rescale[..., None] + own_weight[..., None] * own_value
    attended = (numer / total[..., None]).reshape(stream_count, q_local * HD).astype(jnp.bfloat16)
    partial_out = jnp.dot(attended, w_out, preferred_element_type=jnp.float32)
    share = stream_count // lax.axis_size("tp")
    tp_start = lax.axis_index("tp") * share
    summed = lax.psum_scatter(
        partial_out.astype(jnp.bfloat16), "tp", scatter_dimension=0, tiled=True
    )
    own_hidden = lax.dynamic_slice_in_dim(hidden_float, tp_start, share, 0)
    middle = (own_hidden + summed.astype(jnp.float32)).astype(jnp.bfloat16)
    middle_float = middle.astype(jnp.float32)
    ffn_squares = lax.psum(jnp.sum(middle_float * middle_float, axis=1), "grp")
    ffn_inverse = lax.rsqrt(ffn_squares / D + epsilon)
    normed_own = (middle_float * ffn_inverse[:, None] * ffn_gain).astype(jnp.bfloat16)
    swap = [(0, 1), (1, 0)]
    gate_both = jnp.concatenate([w_gate, lax.ppermute(w_gate, "core", swap)], axis=1)
    up_both = jnp.concatenate([w_up, lax.ppermute(w_up, "core", swap)], axis=1)
    down_both = jnp.concatenate([w_down, lax.ppermute(w_down, "core", swap)], axis=0)
    normed_half = lax.all_gather(normed_own, ("hi", "tp"), axis=0, tiled=True)
    hidden_units = gate_both.shape[1]
    part_gate = jnp.dot(normed_half, gate_both, preferred_element_type=jnp.float32)
    part_upward = jnp.dot(normed_half, up_both, preferred_element_type=jnp.float32)
    both = jnp.concatenate([part_gate, part_upward], axis=1).astype(jnp.bfloat16)
    reduced = lax.psum_scatter(both, "grp", scatter_dimension=0, tiled=True).astype(jnp.float32)
    gate = reduced[:, :hidden_units]
    upward = reduced[:, hidden_units:]
    act = (jax.nn.silu(gate) * upward).astype(jnp.bfloat16)
    act_all = lax.all_gather(act, "grp", axis=0, tiled=True)
    down = jnp.dot(act_all, down_both, preferred_element_type=jnp.float32)
    returned = lax.psum_scatter(
        down.astype(jnp.bfloat16), ("hi", "tp"), scatter_dimension=0, tiled=True
    )
    return (middle_float + returned.astype(jnp.float32)).astype(jnp.bfloat16)


def solution(mesh):
    pool = ("hi", "core")
    chip_mesh = jax.sharding.Mesh(
        mesh.devices.reshape(
            mesh.shape["pool"] // 2, 2, mesh.shape["grp"], mesh.shape["tp"]
        ),
        ("hi", "core", "grp", "tp"),
    )
    return jax.shard_map(
        body,
        mesh=chip_mesh,
        in_specs=(
            P(pool, "grp"),
            P("grp"),
            P("grp", "tp"),
            P("grp", "tp"),
            P("grp", "tp"),
            P("tp", "grp"),
            P(pool, "grp", "tp"),
            P(pool, "grp", "tp"),
            P(pool, "grp", "tp"),
            P(pool, "grp", "tp"),
            P(pool),
            P(pool),
            P("grp"),
            P("grp", pool + ("tp",)),
            P("grp", pool + ("tp",)),
            P(pool + ("tp",), "grp"),
        ),
        out_specs=P(pool + ("tp",), "grp"),
        check_vma=False,
    )
```

```python
import math

import jax
import jax.numpy as jnp
from jax import lax
from jax.sharding import PartitionSpec as P

D = 8192
HD = 128


epsilon = 1e-05


def joined(array, axis, combine):
    everything = jax.tree.map(lambda part: lax.all_gather(part, axis), array)
    first = jax.tree.map(lambda part: part[0], everything)

    def lap(k, so_far):
        return combine(so_far, jax.tree.map(lambda part: part[k], everything))

    return lax.fori_loop(1, lax.axis_size(axis), lap, first)


def combine_parts(earlier, later):
    peak_one, total_one, numer_one = earlier
    peak_two, total_two, numer_two = later
    peak = jnp.maximum(peak_one, peak_two)
    scale_one = jnp.exp(peak_one - peak)
    scale_two = jnp.exp(peak_two - peak)
    total = total_one * scale_one + total_two * scale_two
    numer = numer_one * scale_one[..., None] + numer_two * scale_two[..., None]
    return (peak, total, numer)


def body(
    hidden,
    attn_gain,
    w_query,
    w_key,
    w_value,
    w_out,
    prefix_keys,
    prefix_values,
    suffix_keys,
    suffix_values,
    prefix_ids,
    suffix_lens,
    ffn_gain,
    w_gate,
    w_up,
    w_down,
):
    stream_count = hidden.shape[0]
    hidden_float = hidden.astype(jnp.float32)
    squares = lax.psum(jnp.sum(hidden_float * hidden_float, axis=1), "grp")
    inverse = lax.rsqrt(squares / D + epsilon)
    normed = (hidden_float * inverse[:, None] * attn_gain).astype(jnp.bfloat16)
    part_query = jnp.dot(normed, w_query, preferred_element_type=jnp.float32)
    part_key = jnp.dot(normed, w_key, preferred_element_type=jnp.float32)
    part_value = jnp.dot(normed, w_value, preferred_element_type=jnp.float32)
    query, key_new, value_new = lax.psum((part_query, part_key, part_value), "grp")
    query = query.astype(jnp.bfloat16)
    key_new = key_new.astype(jnp.bfloat16)
    value_new = value_new.astype(jnp.bfloat16)
    kv_local = w_key.shape[1] // HD
    q_local = w_query.shape[1] // HD
    groups = q_local // kv_local
    prefix_local = prefix_keys.shape[0]
    pre_length = prefix_keys.shape[1]
    suf_length = suffix_keys.shape[1]
    factor = 1.0 / math.sqrt(HD)
    heads = query.reshape(stream_count, kv_local, groups, HD)
    pre_key = prefix_keys.reshape(prefix_local, pre_length, kv_local, HD)
    pre_value = prefix_values.reshape(prefix_local, pre_length, kv_local, HD)
    suf_key = suffix_keys.reshape(stream_count, suf_length, kv_local, HD)
    suf_value = suffix_values.reshape(stream_count, suf_length, kv_local, HD)
    pool_index = lax.axis_index("hi") * lax.axis_size("core") + lax.axis_index("core")
    local_prefix = prefix_ids - pool_index * prefix_local
    per_group = stream_count // prefix_local
    one_hot = (local_prefix[:, None] == jnp.arange(prefix_local, dtype=jnp.int32)[None, :]).astype(
        jnp.int32
    )
    rank_within = jnp.sum(jnp.cumsum(one_hot, axis=0) * one_hot, axis=1) - 1
    target = local_prefix * per_group + rank_within
    group_order = (
        jnp.zeros((stream_count,), jnp.int32)
        .at[target]
        .set(jnp.arange(stream_count, dtype=jnp.int32))
    )
    grouped = heads[group_order].reshape(prefix_local, per_group, kv_local, groups, HD)
    pre_scores = (
        jnp.einsum("pskgd,pjkd->pskgj", grouped, pre_key, preferred_element_type=jnp.float32)
        * factor
    )
    pre_peak = pre_scores.max(axis=4).reshape(stream_count, kv_local, groups)[target]
    positions = lax.axis_index("grp") * suf_length + jnp.arange(suf_length, dtype=jnp.int32)
    valid = (positions[None, :] < suffix_lens[:, None])[:, None, None, :]
    suf_scores = (
        jnp.einsum("skgd,sjkd->skgj", heads, suf_key, preferred_element_type=jnp.float32) * factor
    )
    suf_scores = jnp.where(valid, suf_scores, -1e30)
    own_score = (
        jnp.einsum(
            "skgd,skd->skg",
            heads,
            key_new.reshape(stream_count, kv_local, HD),
            preferred_element_type=jnp.float32,
        )
        * factor
    )
    peak = lax.pmax(jnp.maximum(jnp.maximum(pre_peak, suf_scores.max(axis=3)), own_score), "grp")
    peak_grouped = peak[group_order].reshape(prefix_local, per_group, kv_local, groups)
    pre_weights = jnp.exp(pre_scores - peak_grouped[..., None]).astype(jnp.bfloat16)
    unit = jnp.zeros((HD,), pre_value.dtype).at[0].set(1)
    pre_value_ext = jnp.concatenate(
        [pre_value, jnp.broadcast_to(unit, pre_value.shape)], axis=3
    )
    pre_both = jnp.einsum(
        "pskgj,pjkd->pskgd", pre_weights, pre_value_ext, preferred_element_type=jnp.float32
    )
    pre_both = pre_both.reshape(stream_count, kv_local, groups, 2 * HD)[target]
    suf_weights = jnp.where(valid, jnp.exp(suf_scores - peak[:, :, :, None]), 0.0).astype(
        jnp.bfloat16
    )
    total = pre_both[..., HD] + suf_weights.astype(jnp.float32).sum(axis=3)
    numer = pre_both[..., :HD] + jnp.einsum(
        "skgj,sjkd->skgd", suf_weights, suf_value, preferred_element_type=jnp.float32
    )
    flat = stream_count, kv_local * groups
    packed = jnp.concatenate([numer.reshape(stream_count, -1), total.reshape(flat)], axis=1)
    reduced = lax.psum_scatter(packed, "grp", scatter_dimension=0, tiled=True)
    quarter = reduced.shape[0]
    q_start = lax.axis_index("grp") * quarter
    width = kv_local * groups * HD
    numer = reduced[:, :width].reshape(quarter, kv_local, groups, HD)
    total = reduced[:, width:].reshape(quarter, kv_local, groups)
    own_score = lax.dynamic_slice_in_dim(own_score, q_start, quarter, 0)
    own_peak = lax.dynamic_slice_in_dim(peak, q_start, quarter, 0)
    own_weight = jnp.exp(own_score - own_peak).astype(jnp.bfloat16).astype(jnp.float32)
    total = total + own_weight
    own_value = lax.dynamic_slice_in_dim(value_new, q_start, quarter, 0)
    own_value = own_value.reshape(quarter, kv_local, 1, HD).astype(jnp.float32)
    numer = numer + own_weight[..., None] * own_value
    attended = (numer / total[..., None]).reshape(quarter, q_local * HD).astype(jnp.bfloat16)
    attended = lax.all_gather(attended, "grp", axis=0, tiled=True)
    partial_out = jnp.dot(attended, w_out, preferred_element_type=jnp.float32)
    share = stream_count // lax.axis_size("tp")
    tp_start = lax.axis_index("tp") * share
    summed = lax.psum_scatter(
        partial_out.astype(jnp.bfloat16), "tp", scatter_dimension=0, tiled=True
    )
    own_hidden = lax.dynamic_slice_in_dim(hidden_float, tp_start, share, 0)
    middle = (own_hidden + summed.astype(jnp.float32)).astype(jnp.bfloat16)
    middle_float = middle.astype(jnp.float32)
    ffn_squares = lax.psum(jnp.sum(middle_float * middle_float, axis=1), "grp")
    ffn_inverse = lax.rsqrt(ffn_squares / D + epsilon)
    normed_own = (middle_float * ffn_inverse[:, None] * ffn_gain).astype(jnp.bfloat16)
    swap = [(0, 1), (1, 0)]
    gate_both = jnp.concatenate([w_gate, lax.ppermute(w_gate, "core", swap)], axis=1)
    up_both = jnp.concatenate([w_up, lax.ppermute(w_up, "core", swap)], axis=1)
    down_both = jnp.concatenate([w_down, lax.ppermute(w_down, "core", swap)], axis=0)
    normed_half = lax.all_gather(normed_own, ("hi", "tp"), axis=0, tiled=True)
    hidden_units = gate_both.shape[1]
    part_gate = jnp.dot(normed_half, gate_both, preferred_element_type=jnp.float32)
    part_upward = jnp.dot(normed_half, up_both, preferred_element_type=jnp.float32)
    both = jnp.concatenate([part_gate, part_upward], axis=1).astype(jnp.bfloat16)
    reduced = lax.psum_scatter(both, "grp", scatter_dimension=0, tiled=True).astype(jnp.float32)
    gate = reduced[:, :hidden_units]
    upward = reduced[:, hidden_units:]
    act = (jax.nn.silu(gate) * upward).astype(jnp.bfloat16)
    act_all = lax.all_gather(act, "grp", axis=0, tiled=True)
    down = jnp.dot(act_all, down_both, preferred_element_type=jnp.float32)
    returned = lax.psum_scatter(
        down.astype(jnp.bfloat16), ("hi", "tp"), scatter_dimension=0, tiled=True
    )
    return (middle_float + returned.astype(jnp.float32)).astype(jnp.bfloat16)


def solution(mesh):
    pool = ("hi", "core")
    chip_mesh = jax.sharding.Mesh(
        mesh.devices.reshape(
            mesh.shape["pool"] // 2, 2, mesh.shape["grp"], mesh.shape["tp"]
        ),
        ("hi", "core", "grp", "tp"),
    )
    return jax.shard_map(
        body,
        mesh=chip_mesh,
        in_specs=(
            P(pool, "grp"),
            P("grp"),
            P("grp", "tp"),
            P("grp", "tp"),
            P("grp", "tp"),
            P("tp", "grp"),
            P(pool, "grp", "tp"),
            P(pool, "grp", "tp"),
            P(pool, "grp", "tp"),
            P(pool, "grp", "tp"),
            P(pool),
            P(pool),
            P("grp"),
            P("grp", pool + ("tp",)),
            P("grp", pool + ("tp",)),
            P(pool + ("tp",), "grp"),
        ),
        out_specs=P(pool + ("tp",), "grp"),
        check_vma=False,
    )
```

```python
import math

import jax
import jax.numpy as jnp
from jax import lax
from jax.sharding import PartitionSpec as P

D = 8192
HD = 128
TP = ("z", "xlo")


epsilon = 1e-05


def joined(array, axis, combine):
    everything = jax.tree.map(lambda part: lax.all_gather(part, axis), array)
    first = jax.tree.map(lambda part: part[0], everything)

    def lap(k, so_far):
        return combine(so_far, jax.tree.map(lambda part: part[k], everything))

    return lax.fori_loop(1, lax.axis_size(axis), lap, first)


def combine_parts(earlier, later):
    peak_one, total_one, numer_one = earlier
    peak_two, total_two, numer_two = later
    peak = jnp.maximum(peak_one, peak_two)
    scale_one = jnp.exp(peak_one - peak)
    scale_two = jnp.exp(peak_two - peak)
    total = total_one * scale_one + total_two * scale_two
    numer = numer_one * scale_one[..., None] + numer_two * scale_two[..., None]
    return (peak, total, numer)


def body(
    hidden,
    attn_gain,
    w_query,
    w_key,
    w_value,
    w_out,
    prefix_keys,
    prefix_values,
    suffix_keys,
    suffix_values,
    prefix_ids,
    suffix_lens,
    ffn_gain,
    w_gate,
    w_up,
    w_down,
):
    stream_count = hidden.shape[0]
    hidden_float = hidden.astype(jnp.float32)
    squares = lax.psum(jnp.sum(hidden_float * hidden_float, axis=1), "grp")
    inverse = lax.rsqrt(squares / D + epsilon)
    normed = (hidden_float * inverse[:, None] * attn_gain).astype(jnp.bfloat16)
    part_query = jnp.dot(normed, w_query, preferred_element_type=jnp.float32)
    part_key = jnp.dot(normed, w_key, preferred_element_type=jnp.float32)
    part_value = jnp.dot(normed, w_value, preferred_element_type=jnp.float32)
    query, key_new, value_new = lax.psum((part_query, part_key, part_value), "grp")
    query = query.astype(jnp.bfloat16)
    key_new = key_new.astype(jnp.bfloat16)
    value_new = value_new.astype(jnp.bfloat16)
    kv_local = w_key.shape[1] // HD
    q_local = w_query.shape[1] // HD
    groups = q_local // kv_local
    prefix_local = prefix_keys.shape[0]
    pre_length = prefix_keys.shape[1]
    suf_length = suffix_keys.shape[1]
    factor = 1.0 / math.sqrt(HD)
    heads = query.reshape(stream_count, kv_local, groups, HD)
    pre_key = prefix_keys.reshape(prefix_local, pre_length, kv_local, HD)
    pre_value = prefix_values.reshape(prefix_local, pre_length, kv_local, HD)
    suf_key = suffix_keys.reshape(stream_count, suf_length, kv_local, HD)
    suf_value = suffix_values.reshape(stream_count, suf_length, kv_local, HD)
    pool_index = lax.axis_index("hi") * lax.axis_size("core") + lax.axis_index("core")
    local_prefix = prefix_ids - pool_index * prefix_local
    per_group = stream_count // prefix_local
    one_hot = (local_prefix[:, None] == jnp.arange(prefix_local, dtype=jnp.int32)[None, :]).astype(
        jnp.int32
    )
    rank_within = jnp.sum(jnp.cumsum(one_hot, axis=0) * one_hot, axis=1) - 1
    target = local_prefix * per_group + rank_within
    group_order = (
        jnp.zeros((stream_count,), jnp.int32)
        .at[target]
        .set(jnp.arange(stream_count, dtype=jnp.int32))
    )
    grouped = heads[group_order].reshape(prefix_local, per_group, kv_local, groups, HD)
    pre_scores = (
        jnp.einsum("pskgd,pjkd->pskgj", grouped, pre_key, preferred_element_type=jnp.float32)
        * factor
    )
    pre_peak = pre_scores.max(axis=4).reshape(stream_count, kv_local, groups)[target]
    positions = lax.axis_index("grp") * suf_length + jnp.arange(suf_length, dtype=jnp.int32)
    valid = (positions[None, :] < suffix_lens[:, None])[:, None, None, :]
    suf_scores = (
        jnp.einsum("skgd,sjkd->skgj", heads, suf_key, preferred_element_type=jnp.float32) * factor
    )
    suf_scores = jnp.where(valid, suf_scores, -1e30)
    own_score = (
        jnp.einsum(
            "skgd,skd->skg",
            heads,
            key_new.reshape(stream_count, kv_local, HD),
            preferred_element_type=jnp.float32,
        )
        * factor
    )
    peak = lax.pmax(jnp.maximum(jnp.maximum(pre_peak, suf_scores.max(axis=3)), own_score), "grp")
    peak_grouped = peak[group_order].reshape(prefix_local, per_group, kv_local, groups)
    pre_weights = jnp.exp(pre_scores - peak_grouped[..., None]).astype(jnp.bfloat16)
    unit = jnp.zeros((HD,), pre_value.dtype).at[0].set(1)
    pre_value_ext = jnp.concatenate(
        [pre_value, jnp.broadcast_to(unit, pre_value.shape)], axis=3
    )
    pre_both = jnp.einsum(
        "pskgj,pjkd->pskgd", pre_weights, pre_value_ext, preferred_element_type=jnp.float32
    )
    pre_both = pre_both.reshape(stream_count, kv_local, groups, 2 * HD)[target]
    suf_weights = jnp.where(valid, jnp.exp(suf_scores - peak[:, :, :, None]), 0.0).astype(
        jnp.bfloat16
    )
    total = pre_both[..., HD] + suf_weights.astype(jnp.float32).sum(axis=3)
    numer = pre_both[..., :HD] + jnp.einsum(
        "skgj,sjkd->skgd", suf_weights, suf_value, preferred_element_type=jnp.float32
    )
    flat = stream_count, kv_local * groups
    packed = jnp.concatenate([numer.reshape(stream_count, -1), total.reshape(flat)], axis=1)
    reduced = lax.psum_scatter(packed, "grp", scatter_dimension=0, tiled=True)
    quarter = reduced.shape[0]
    q_start = lax.axis_index("grp") * quarter
    width = kv_local * groups * HD
    numer = reduced[:, :width].reshape(quarter, kv_local, groups, HD)
    total = reduced[:, width:].reshape(quarter, kv_local, groups)
    own_score = lax.dynamic_slice_in_dim(own_score, q_start, quarter, 0)
    own_peak = lax.dynamic_slice_in_dim(peak, q_start, quarter, 0)
    own_weight = jnp.exp(own_score - own_peak).astype(jnp.bfloat16).astype(jnp.float32)
    total = total + own_weight
    own_value = lax.dynamic_slice_in_dim(value_new, q_start, quarter, 0)
    own_value = own_value.reshape(quarter, kv_local, 1, HD).astype(jnp.float32)
    numer = numer + own_weight[..., None] * own_value
    attended = (numer / total[..., None]).reshape(quarter, q_local * HD).astype(jnp.bfloat16)
    attended = lax.all_gather(attended, "grp", axis=0, tiled=True)
    partial_out = jnp.dot(attended, w_out, preferred_element_type=jnp.float32)
    share = stream_count // (lax.axis_size("z") * lax.axis_size("xlo"))
    tp_start = (lax.axis_index("z") * lax.axis_size("xlo") + lax.axis_index("xlo")) * share
    summed = lax.psum_scatter(
        partial_out.astype(jnp.bfloat16), TP, scatter_dimension=0, tiled=True
    )
    own_hidden = lax.dynamic_slice_in_dim(hidden_float, tp_start, share, 0)
    middle = (own_hidden + summed.astype(jnp.float32)).astype(jnp.bfloat16)
    middle_float = middle.astype(jnp.float32)
    ffn_squares = lax.psum(jnp.sum(middle_float * middle_float, axis=1), "grp")
    ffn_inverse = lax.rsqrt(ffn_squares / D + epsilon)
    normed_own = (middle_float * ffn_inverse[:, None] * ffn_gain).astype(jnp.bfloat16)
    swap = [(0, 1), (1, 0)]
    gate_both = jnp.concatenate([w_gate, lax.ppermute(w_gate, "core", swap)], axis=1)
    up_both = jnp.concatenate([w_up, lax.ppermute(w_up, "core", swap)], axis=1)
    down_both = jnp.concatenate([w_down, lax.ppermute(w_down, "core", swap)], axis=0)
    normed_row = lax.all_gather(normed_own, ("hi", "xlo"), axis=0, tiled=True)
    normed_half = lax.all_gather(normed_row, "z", axis=0, tiled=True)
    hidden_units = gate_both.shape[1]
    part_gate = jnp.dot(normed_half, gate_both, preferred_element_type=jnp.float32)
    part_upward = jnp.dot(normed_half, up_both, preferred_element_type=jnp.float32)
    both = jnp.concatenate([part_gate, part_upward], axis=1).astype(jnp.bfloat16)
    reduced = lax.psum_scatter(both, "grp", scatter_dimension=0, tiled=True).astype(jnp.float32)
    gate = reduced[:, :hidden_units]
    upward = reduced[:, hidden_units:]
    act = (jax.nn.silu(gate) * upward).astype(jnp.bfloat16)
    act_all = lax.all_gather(act, "grp", axis=0, tiled=True)
    down = jnp.dot(act_all, down_both, preferred_element_type=jnp.float32)
    returned = lax.psum_scatter(down.astype(jnp.bfloat16), "z", scatter_dimension=0, tiled=True)
    returned = lax.psum_scatter(returned, ("hi", "xlo"), scatter_dimension=0, tiled=True)
    return (middle_float + returned.astype(jnp.float32)).astype(jnp.bfloat16)


def solution(mesh):
    pool = ("hi", "core")
    chip_mesh = jax.sharding.Mesh(
        mesh.devices.reshape(
            mesh.shape["pool"] // 2, 2, mesh.shape["grp"], mesh.shape["tp"] // 2, 2
        ),
        ("hi", "core", "grp", "z", "xlo"),
    )
    return jax.shard_map(
        body,
        mesh=chip_mesh,
        in_specs=(
            P(pool, "grp"),
            P("grp"),
            P("grp", TP),
            P("grp", TP),
            P("grp", TP),
            P(TP, "grp"),
            P(pool, "grp", TP),
            P(pool, "grp", TP),
            P(pool, "grp", TP),
            P(pool, "grp", TP),
            P(pool),
            P(pool),
            P("grp"),
            P("grp", pool + TP),
            P("grp", pool + TP),
            P(pool + TP, "grp"),
        ),
        out_specs=P(pool + TP, "grp"),
        check_vma=False,
    )
```

```python
import math

import jax
import jax.numpy as jnp
from jax import lax
from jax.sharding import PartitionSpec as P

D = 8192
HD = 128
TP = ("z", "xlo")


epsilon = 1e-05


def joined(array, axis, combine):
    everything = jax.tree.map(lambda part: lax.all_gather(part, axis), array)
    first = jax.tree.map(lambda part: part[0], everything)

    def lap(k, so_far):
        return combine(so_far, jax.tree.map(lambda part: part[k], everything))

    return lax.fori_loop(1, lax.axis_size(axis), lap, first)


def combine_parts(earlier, later):
    peak_one, total_one, numer_one = earlier
    peak_two, total_two, numer_two = later
    peak = jnp.maximum(peak_one, peak_two)
    scale_one = jnp.exp(peak_one - peak)
    scale_two = jnp.exp(peak_two - peak)
    total = total_one * scale_one + total_two * scale_two
    numer = numer_one * scale_one[..., None] + numer_two * scale_two[..., None]
    return (peak, total, numer)


def body(
    hidden,
    attn_gain,
    w_query,
    w_key,
    w_value,
    w_out,
    prefix_keys,
    prefix_values,
    suffix_keys,
    suffix_values,
    prefix_ids,
    suffix_lens,
    ffn_gain,
    w_gate,
    w_up,
    w_down,
):
    stream_count = hidden.shape[0]
    hidden_float = hidden.astype(jnp.float32)
    squares = lax.psum(jnp.sum(hidden_float * hidden_float, axis=1), "grp")
    inverse = lax.rsqrt(squares / D + epsilon)
    normed = (hidden_float * inverse[:, None] * attn_gain).astype(jnp.bfloat16)
    part_query = jnp.dot(normed, w_query, preferred_element_type=jnp.float32)
    part_key = jnp.dot(normed, w_key, preferred_element_type=jnp.float32)
    part_value = jnp.dot(normed, w_value, preferred_element_type=jnp.float32)
    query, key_new, value_new = lax.psum((part_query, part_key, part_value), "grp")
    query = query.astype(jnp.bfloat16)
    key_new = key_new.astype(jnp.bfloat16)
    value_new = value_new.astype(jnp.bfloat16)
    kv_local = w_key.shape[1] // HD
    q_local = w_query.shape[1] // HD
    groups = q_local // kv_local
    prefix_local = prefix_keys.shape[0]
    pre_length = prefix_keys.shape[1]
    suf_length = suffix_keys.shape[1]
    factor = 1.0 / math.sqrt(HD)
    heads = query.reshape(stream_count, kv_local, groups, HD)
    pre_key = prefix_keys.reshape(prefix_local, pre_length, kv_local, HD)
    pre_value = prefix_values.reshape(prefix_local, pre_length, kv_local, HD)
    suf_key = suffix_keys.reshape(stream_count, suf_length, kv_local, HD)
    suf_value = suffix_values.reshape(stream_count, suf_length, kv_local, HD)
    pool_index = lax.axis_index("hi") * lax.axis_size("core") + lax.axis_index("core")
    local_prefix = prefix_ids - pool_index * prefix_local
    per_group = stream_count // prefix_local
    one_hot = (local_prefix[:, None] == jnp.arange(prefix_local, dtype=jnp.int32)[None, :]).astype(
        jnp.int32
    )
    rank_within = jnp.sum(jnp.cumsum(one_hot, axis=0) * one_hot, axis=1) - 1
    target = local_prefix * per_group + rank_within
    group_order = (
        jnp.zeros((stream_count,), jnp.int32)
        .at[target]
        .set(jnp.arange(stream_count, dtype=jnp.int32))
    )
    grouped = heads[group_order].reshape(prefix_local, per_group, kv_local, groups, HD)
    pre_scores = (
        jnp.einsum("pskgd,pjkd->pskgj", grouped, pre_key, preferred_element_type=jnp.float32)
        * factor
    )
    pre_peak = pre_scores.max(axis=4).reshape(stream_count, kv_local, groups)[target]
    positions = lax.axis_index("grp") * suf_length + jnp.arange(suf_length, dtype=jnp.int32)
    valid = (positions[None, :] < suffix_lens[:, None])[:, None, None, :]
    suf_scores = (
        jnp.einsum("skgd,sjkd->skgj", heads, suf_key, preferred_element_type=jnp.float32) * factor
    )
    suf_scores = jnp.where(valid, suf_scores, -1e30)
    own_score = (
        jnp.einsum(
            "skgd,skd->skg",
            heads,
            key_new.reshape(stream_count, kv_local, HD),
            preferred_element_type=jnp.float32,
        )
        * factor
    )
    peak = lax.pmax(jnp.maximum(jnp.maximum(pre_peak, suf_scores.max(axis=3)), own_score), "grp")
    peak_grouped = peak[group_order].reshape(prefix_local, per_group, kv_local, groups)
    pre_weights = jnp.exp(pre_scores - peak_grouped[..., None]).astype(jnp.bfloat16)
    unit = jnp.zeros((HD,), pre_value.dtype).at[0].set(1)
    pre_value_ext = jnp.concatenate(
        [pre_value, jnp.broadcast_to(unit, pre_value.shape)], axis=3
    )
    pre_both = jnp.einsum(
        "pskgj,pjkd->pskgd", pre_weights, pre_value_ext, preferred_element_type=jnp.float32
    )
    pre_both = pre_both.reshape(stream_count, kv_local, groups, 2 * HD)[target]
    suf_weights = jnp.where(valid, jnp.exp(suf_scores - peak[:, :, :, None]), 0.0).astype(
        jnp.bfloat16
    )
    total = pre_both[..., HD] + suf_weights.astype(jnp.float32).sum(axis=3)
    numer = pre_both[..., :HD] + jnp.einsum(
        "skgj,sjkd->skgd", suf_weights, suf_value, preferred_element_type=jnp.float32
    )
    flat = stream_count, kv_local * groups
    packed = jnp.concatenate([numer.reshape(stream_count, -1), total.reshape(flat)], axis=1)
    reduced = lax.psum(packed, "grp")
    width = kv_local * groups * HD
    numer = reduced[:, :width].reshape(stream_count, kv_local, groups, HD)
    total = reduced[:, width:].reshape(stream_count, kv_local, groups)
    own_weight = jnp.exp(own_score - peak).astype(jnp.bfloat16).astype(jnp.float32)
    total = total + own_weight
    own_value = value_new.reshape(stream_count, kv_local, 1, HD).astype(jnp.float32)
    numer = numer + own_weight[..., None] * own_value
    attended = (numer / total[..., None]).reshape(stream_count, q_local * HD).astype(jnp.bfloat16)
    partial_out = jnp.dot(attended, w_out, preferred_element_type=jnp.float32)
    share = stream_count // (lax.axis_size("z") * lax.axis_size("xlo"))
    tp_start = (lax.axis_index("z") * lax.axis_size("xlo") + lax.axis_index("xlo")) * share
    summed = lax.psum_scatter(
        partial_out.astype(jnp.bfloat16), TP, scatter_dimension=0, tiled=True
    )
    own_hidden = lax.dynamic_slice_in_dim(hidden_float, tp_start, share, 0)
    middle = (own_hidden + summed.astype(jnp.float32)).astype(jnp.bfloat16)
    middle_float = middle.astype(jnp.float32)
    ffn_squares = lax.psum(jnp.sum(middle_float * middle_float, axis=1), "grp")
    ffn_inverse = lax.rsqrt(ffn_squares / D + epsilon)
    normed_own = (middle_float * ffn_inverse[:, None] * ffn_gain).astype(jnp.bfloat16)
    swap = [(0, 1), (1, 0)]
    gate_both = jnp.concatenate([w_gate, lax.ppermute(w_gate, "core", swap)], axis=1)
    up_both = jnp.concatenate([w_up, lax.ppermute(w_up, "core", swap)], axis=1)
    down_both = jnp.concatenate([w_down, lax.ppermute(w_down, "core", swap)], axis=0)
    normed_row = lax.all_gather(normed_own, ("hi", "xlo"), axis=0, tiled=True)
    normed_half = lax.all_gather(normed_row, "z", axis=0, tiled=True)
    hidden_units = gate_both.shape[1]
    part_gate = jnp.dot(normed_half, gate_both, preferred_element_type=jnp.float32)
    part_upward = jnp.dot(normed_half, up_both, preferred_element_type=jnp.float32)
    both = jnp.concatenate([part_gate, part_upward], axis=1).astype(jnp.bfloat16)
    reduced = lax.psum(both, "grp").astype(jnp.float32)
    gate = reduced[:, :hidden_units]
    upward = reduced[:, hidden_units:]
    act = (jax.nn.silu(gate) * upward).astype(jnp.bfloat16)
    down = jnp.dot(act, down_both, preferred_element_type=jnp.float32)
    returned = lax.psum_scatter(down.astype(jnp.bfloat16), "z", scatter_dimension=0, tiled=True)
    returned = lax.psum_scatter(returned, ("hi", "xlo"), scatter_dimension=0, tiled=True)
    return (middle_float + returned.astype(jnp.float32)).astype(jnp.bfloat16)


def solution(mesh):
    pool = ("hi", "core")
    chip_mesh = jax.sharding.Mesh(
        mesh.devices.reshape(
            mesh.shape["pool"] // 2, 2, mesh.shape["grp"], mesh.shape["tp"] // 2, 2
        ),
        ("hi", "core", "grp", "z", "xlo"),
    )
    return jax.shard_map(
        body,
        mesh=chip_mesh,
        in_specs=(
            P(pool, "grp"),
            P("grp"),
            P("grp", TP),
            P("grp", TP),
            P("grp", TP),
            P(TP, "grp"),
            P(pool, "grp", TP),
            P(pool, "grp", TP),
            P(pool, "grp", TP),
            P(pool, "grp", TP),
            P(pool),
            P(pool),
            P("grp"),
            P("grp", pool + TP),
            P("grp", pool + TP),
            P(pool + TP, "grp"),
        ),
        out_specs=P(pool + TP, "grp"),
        check_vma=False,
    )
```

```python
import math

import jax
import jax.numpy as jnp
from jax import lax
from jax.sharding import PartitionSpec as P

D = 8192
HD = 128
TP = ("z", "xlo")


epsilon = 1e-05


def joined(array, axis, combine):
    everything = jax.tree.map(lambda part: lax.all_gather(part, axis), array)
    first = jax.tree.map(lambda part: part[0], everything)

    def lap(k, so_far):
        return combine(so_far, jax.tree.map(lambda part: part[k], everything))

    return lax.fori_loop(1, lax.axis_size(axis), lap, first)


def combine_parts(earlier, later):
    peak_one, total_one, numer_one = earlier
    peak_two, total_two, numer_two = later
    peak = jnp.maximum(peak_one, peak_two)
    scale_one = jnp.exp(peak_one - peak)
    scale_two = jnp.exp(peak_two - peak)
    total = total_one * scale_one + total_two * scale_two
    numer = numer_one * scale_one[..., None] + numer_two * scale_two[..., None]
    return (peak, total, numer)


def pair_gather(part, axis):
    swap = [(0, 1), (1, 0)]
    other = lax.ppermute(part, axis, swap)
    first = lax.axis_index(axis) == 0
    return jnp.where(
        first, jnp.concatenate([part, other], axis=0), jnp.concatenate([other, part], axis=0)
    )


def pair_reduce(rows, axis):
    swap = [(0, 1), (1, 0)]
    index = lax.axis_index(axis)
    halves = rows.reshape((2, rows.shape[0] // 2) + rows.shape[1:])
    mine = lax.dynamic_index_in_dim(halves, index, 0, keepdims=False)
    other = lax.dynamic_index_in_dim(halves, 1 - index, 0, keepdims=False)
    other = lax.ppermute(other.astype(jnp.bfloat16), axis, swap)
    return mine.astype(jnp.float32) + other.astype(jnp.float32)


def body(
    hidden,
    attn_gain,
    w_query,
    w_key,
    w_value,
    w_out,
    prefix_keys,
    prefix_values,
    suffix_keys,
    suffix_values,
    prefix_ids,
    suffix_lens,
    ffn_gain,
    w_gate,
    w_up,
    w_down,
):
    stream_count = hidden.shape[0]
    hidden_float = hidden.astype(jnp.float32)
    squares = lax.psum(jnp.sum(hidden_float * hidden_float, axis=1), "grp")
    inverse = lax.rsqrt(squares / D + epsilon)
    normed = (hidden_float * inverse[:, None] * attn_gain).astype(jnp.bfloat16)
    part_query = jnp.dot(normed, w_query, preferred_element_type=jnp.float32)
    part_key = jnp.dot(normed, w_key, preferred_element_type=jnp.float32)
    part_value = jnp.dot(normed, w_value, preferred_element_type=jnp.float32)
    query, key_new, value_new = lax.psum((part_query, part_key, part_value), "grp")
    query = query.astype(jnp.bfloat16)
    key_new = key_new.astype(jnp.bfloat16)
    value_new = value_new.astype(jnp.bfloat16)
    kv_local = w_key.shape[1] // HD
    q_local = w_query.shape[1] // HD
    groups = q_local // kv_local
    prefix_local = prefix_keys.shape[0]
    pre_length = prefix_keys.shape[1]
    suf_length = suffix_keys.shape[1]
    factor = 1.0 / math.sqrt(HD)
    heads = query.reshape(stream_count, kv_local, groups, HD)
    pre_key = prefix_keys.reshape(prefix_local, pre_length, kv_local, HD)
    pre_value = prefix_values.reshape(prefix_local, pre_length, kv_local, HD)
    suf_key = suffix_keys.reshape(stream_count, suf_length, kv_local, HD)
    suf_value = suffix_values.reshape(stream_count, suf_length, kv_local, HD)
    pool_index = lax.axis_index("hi") * lax.axis_size("core") + lax.axis_index("core")
    local_prefix = prefix_ids - pool_index * prefix_local
    per_group = stream_count // prefix_local
    one_hot = (local_prefix[:, None] == jnp.arange(prefix_local, dtype=jnp.int32)[None, :]).astype(
        jnp.int32
    )
    rank_within = jnp.sum(jnp.cumsum(one_hot, axis=0) * one_hot, axis=1) - 1
    target = local_prefix * per_group + rank_within
    group_order = (
        jnp.zeros((stream_count,), jnp.int32)
        .at[target]
        .set(jnp.arange(stream_count, dtype=jnp.int32))
    )
    grouped = heads[group_order].reshape(prefix_local, per_group, kv_local, groups, HD)
    pre_scores = (
        jnp.einsum("pskgd,pjkd->pskgj", grouped, pre_key, preferred_element_type=jnp.float32)
        * factor
    )
    pre_peak = pre_scores.max(axis=4).reshape(stream_count, kv_local, groups)[target]
    positions = lax.axis_index("grp") * suf_length + jnp.arange(suf_length, dtype=jnp.int32)
    valid = (positions[None, :] < suffix_lens[:, None])[:, None, None, :]
    suf_scores = (
        jnp.einsum("skgd,sjkd->skgj", heads, suf_key, preferred_element_type=jnp.float32) * factor
    )
    suf_scores = jnp.where(valid, suf_scores, -1e30)
    own_score = (
        jnp.einsum(
            "skgd,skd->skg",
            heads,
            key_new.reshape(stream_count, kv_local, HD),
            preferred_element_type=jnp.float32,
        )
        * factor
    )
    peak = lax.pmax(jnp.maximum(jnp.maximum(pre_peak, suf_scores.max(axis=3)), own_score), "grp")
    peak_grouped = peak[group_order].reshape(prefix_local, per_group, kv_local, groups)
    pre_weights = jnp.exp(pre_scores - peak_grouped[..., None]).astype(jnp.bfloat16)
    unit = jnp.zeros((HD,), pre_value.dtype).at[0].set(1)
    pre_value_ext = jnp.concatenate(
        [pre_value, jnp.broadcast_to(unit, pre_value.shape)], axis=3
    )
    pre_both = jnp.einsum(
        "pskgj,pjkd->pskgd", pre_weights, pre_value_ext, preferred_element_type=jnp.float32
    )
    pre_both = pre_both.reshape(stream_count, kv_local, groups, 2 * HD)[target]
    suf_weights = jnp.where(valid, jnp.exp(suf_scores - peak[:, :, :, None]), 0.0).astype(
        jnp.bfloat16
    )
    total = pre_both[..., HD] + suf_weights.astype(jnp.float32).sum(axis=3)
    numer = pre_both[..., :HD] + jnp.einsum(
        "skgj,sjkd->skgd", suf_weights, suf_value, preferred_element_type=jnp.float32
    )
    flat = stream_count, kv_local * groups
    packed = jnp.concatenate([numer.reshape(stream_count, -1), total.reshape(flat)], axis=1)
    reduced = lax.psum_scatter(packed, "grp", scatter_dimension=0, tiled=True)
    quarter = reduced.shape[0]
    q_start = lax.axis_index("grp") * quarter
    width = kv_local * groups * HD
    numer = reduced[:, :width].reshape(quarter, kv_local, groups, HD)
    total = reduced[:, width:].reshape(quarter, kv_local, groups)
    own_score = lax.dynamic_slice_in_dim(own_score, q_start, quarter, 0)
    own_peak = lax.dynamic_slice_in_dim(peak, q_start, quarter, 0)
    own_weight = jnp.exp(own_score - own_peak).astype(jnp.bfloat16).astype(jnp.float32)
    total = total + own_weight
    own_value = lax.dynamic_slice_in_dim(value_new, q_start, quarter, 0)
    own_value = own_value.reshape(quarter, kv_local, 1, HD).astype(jnp.float32)
    numer = numer + own_weight[..., None] * own_value
    attended = (numer / total[..., None]).reshape(quarter, q_local * HD).astype(jnp.bfloat16)
    attended = lax.all_gather(attended, "grp", axis=0, tiled=True)
    partial_out = jnp.dot(attended, w_out, preferred_element_type=jnp.float32)
    share = stream_count // (lax.axis_size("z") * lax.axis_size("xlo"))
    tp_start = (lax.axis_index("z") * lax.axis_size("xlo") + lax.axis_index("xlo")) * share
    summed = lax.psum_scatter(
        partial_out.astype(jnp.bfloat16), "z", scatter_dimension=0, tiled=True
    )
    summed = pair_reduce(summed, "xlo")
    own_hidden = lax.dynamic_slice_in_dim(hidden_float, tp_start, share, 0)
    middle = (own_hidden + summed.astype(jnp.float32)).astype(jnp.bfloat16)
    middle_float = middle.astype(jnp.float32)
    ffn_squares = lax.psum(jnp.sum(middle_float * middle_float, axis=1), "grp")
    ffn_inverse = lax.rsqrt(ffn_squares / D + epsilon)
    normed_own = (middle_float * ffn_inverse[:, None] * ffn_gain).astype(jnp.bfloat16)
    swap = [(0, 1), (1, 0)]
    gate_both = jnp.concatenate([w_gate, lax.ppermute(w_gate, "core", swap)], axis=1)
    up_both = jnp.concatenate([w_up, lax.ppermute(w_up, "core", swap)], axis=1)
    down_both = jnp.concatenate([w_down, lax.ppermute(w_down, "core", swap)], axis=0)
    normed_row = pair_gather(pair_gather(normed_own, "xlo"), "hi")
    normed_half = lax.all_gather(normed_row, "z", axis=0, tiled=True)
    hidden_units = gate_both.shape[1]
    part_gate = jnp.dot(normed_half, gate_both, preferred_element_type=jnp.float32)
    part_upward = jnp.dot(normed_half, up_both, preferred_element_type=jnp.float32)
    both = jnp.concatenate([part_gate, part_upward], axis=1).astype(jnp.bfloat16)
    reduced = lax.psum_scatter(both, "grp", scatter_dimension=0, tiled=True).astype(jnp.float32)
    gate = reduced[:, :hidden_units]
    upward = reduced[:, hidden_units:]
    act = (jax.nn.silu(gate) * upward).astype(jnp.bfloat16)
    act_all = lax.all_gather(act, "grp", axis=0, tiled=True)
    down = jnp.dot(act_all, down_both, preferred_element_type=jnp.float32)
    returned = lax.psum_scatter(down.astype(jnp.bfloat16), "z", scatter_dimension=0, tiled=True)
    returned = pair_reduce(pair_reduce(returned, "hi").astype(jnp.bfloat16), "xlo")
    return (middle_float + returned.astype(jnp.float32)).astype(jnp.bfloat16)


def solution(mesh):
    pool = ("hi", "core")
    chip_mesh = jax.sharding.Mesh(
        mesh.devices.reshape(
            mesh.shape["pool"] // 2, 2, mesh.shape["grp"], mesh.shape["tp"] // 2, 2
        ),
        ("hi", "core", "grp", "z", "xlo"),
    )
    return jax.shard_map(
        body,
        mesh=chip_mesh,
        in_specs=(
            P(pool, "grp"),
            P("grp"),
            P("grp", TP),
            P("grp", TP),
            P("grp", TP),
            P(TP, "grp"),
            P(pool, "grp", TP),
            P(pool, "grp", TP),
            P(pool, "grp", TP),
            P(pool, "grp", TP),
            P(pool),
            P(pool),
            P("grp"),
            P("grp", pool + TP),
            P("grp", pool + TP),
            P(pool + TP, "grp"),
        ),
        out_specs=P(pool + TP, "grp"),
        check_vma=False,
    )
```

```python
import math

import jax
import jax.numpy as jnp
from jax import lax
from jax.sharding import PartitionSpec as P

D = 8192
HD = 128
TP = ("z", "xlo")


epsilon = 1e-05


def joined(array, axis, combine):
    everything = jax.tree.map(lambda part: lax.all_gather(part, axis), array)
    first = jax.tree.map(lambda part: part[0], everything)

    def lap(k, so_far):
        return combine(so_far, jax.tree.map(lambda part: part[k], everything))

    return lax.fori_loop(1, lax.axis_size(axis), lap, first)


def combine_parts(earlier, later):
    peak_one, total_one, numer_one = earlier
    peak_two, total_two, numer_two = later
    peak = jnp.maximum(peak_one, peak_two)
    scale_one = jnp.exp(peak_one - peak)
    scale_two = jnp.exp(peak_two - peak)
    total = total_one * scale_one + total_two * scale_two
    numer = numer_one * scale_one[..., None] + numer_two * scale_two[..., None]
    return (peak, total, numer)


def pair_gather(part, axis):
    swap = [(0, 1), (1, 0)]
    other = lax.ppermute(part, axis, swap)
    first = lax.axis_index(axis) == 0
    return jnp.where(
        first, jnp.concatenate([part, other], axis=0), jnp.concatenate([other, part], axis=0)
    )


def pair_reduce(rows, axis):
    swap = [(0, 1), (1, 0)]
    index = lax.axis_index(axis)
    halves = rows.reshape((2, rows.shape[0] // 2) + rows.shape[1:])
    mine = lax.dynamic_index_in_dim(halves, index, 0, keepdims=False)
    other = lax.dynamic_index_in_dim(halves, 1 - index, 0, keepdims=False)
    other = lax.ppermute(other.astype(jnp.bfloat16), axis, swap)
    return mine.astype(jnp.float32) + other.astype(jnp.float32)


def ring_gather(part, axis):
    size = lax.axis_size(axis)
    index = lax.axis_index(axis)
    pieces = [part]
    for shift in range(1, size):
        pairs = [(i, (i + shift) % size) for i in range(size)]
        pieces.append(lax.ppermute(part, axis, pairs))
    stacked = jnp.stack(pieces)
    order = (index - jnp.arange(size, dtype=jnp.int32)) % size
    return stacked[order].reshape((size * part.shape[0],) + part.shape[1:])


def ring_reduce(rows, axis):
    size = lax.axis_size(axis)
    index = lax.axis_index(axis)
    blocks = rows.reshape((size, rows.shape[0] // size) + rows.shape[1:])
    total = lax.dynamic_index_in_dim(blocks, index, 0, keepdims=False).astype(jnp.float32)
    for shift in range(1, size):
        pairs = [(i, (i + shift) % size) for i in range(size)]
        outgoing = lax.dynamic_index_in_dim(blocks, (index + shift) % size, 0, keepdims=False)
        total = total + lax.ppermute(outgoing, axis, pairs).astype(jnp.float32)
    return total


def body(
    hidden,
    attn_gain,
    w_query,
    w_key,
    w_value,
    w_out,
    prefix_keys,
    prefix_values,
    suffix_keys,
    suffix_values,
    prefix_ids,
    suffix_lens,
    ffn_gain,
    w_gate,
    w_up,
    w_down,
):
    stream_count = hidden.shape[0]
    hidden_float = hidden.astype(jnp.float32)
    squares = lax.psum(jnp.sum(hidden_float * hidden_float, axis=1), "grp")
    inverse = lax.rsqrt(squares / D + epsilon)
    normed = (hidden_float * inverse[:, None] * attn_gain).astype(jnp.bfloat16)
    part_query = jnp.dot(normed, w_query, preferred_element_type=jnp.float32)
    part_key = jnp.dot(normed, w_key, preferred_element_type=jnp.float32)
    part_value = jnp.dot(normed, w_value, preferred_element_type=jnp.float32)
    query, key_new, value_new = lax.psum((part_query, part_key, part_value), "grp")
    query = query.astype(jnp.bfloat16)
    key_new = key_new.astype(jnp.bfloat16)
    value_new = value_new.astype(jnp.bfloat16)
    kv_local = w_key.shape[1] // HD
    q_local = w_query.shape[1] // HD
    groups = q_local // kv_local
    prefix_local = prefix_keys.shape[0]
    pre_length = prefix_keys.shape[1]
    suf_length = suffix_keys.shape[1]
    factor = 1.0 / math.sqrt(HD)
    heads = query.reshape(stream_count, kv_local, groups, HD)
    pre_key = prefix_keys.reshape(prefix_local, pre_length, kv_local, HD)
    pre_value = prefix_values.reshape(prefix_local, pre_length, kv_local, HD)
    suf_key = suffix_keys.reshape(stream_count, suf_length, kv_local, HD)
    suf_value = suffix_values.reshape(stream_count, suf_length, kv_local, HD)
    pool_index = lax.axis_index("hi") * lax.axis_size("core") + lax.axis_index("core")
    local_prefix = prefix_ids - pool_index * prefix_local
    per_group = stream_count // prefix_local
    one_hot = (local_prefix[:, None] == jnp.arange(prefix_local, dtype=jnp.int32)[None, :]).astype(
        jnp.int32
    )
    rank_within = jnp.sum(jnp.cumsum(one_hot, axis=0) * one_hot, axis=1) - 1
    target = local_prefix * per_group + rank_within
    group_order = (
        jnp.zeros((stream_count,), jnp.int32)
        .at[target]
        .set(jnp.arange(stream_count, dtype=jnp.int32))
    )
    grouped = heads[group_order].reshape(prefix_local, per_group, kv_local, groups, HD)
    pre_scores = (
        jnp.einsum("pskgd,pjkd->pskgj", grouped, pre_key, preferred_element_type=jnp.float32)
        * factor
    )
    pre_peak = pre_scores.max(axis=4).reshape(stream_count, kv_local, groups)[target]
    positions = lax.axis_index("grp") * suf_length + jnp.arange(suf_length, dtype=jnp.int32)
    valid = (positions[None, :] < suffix_lens[:, None])[:, None, None, :]
    suf_scores = (
        jnp.einsum("skgd,sjkd->skgj", heads, suf_key, preferred_element_type=jnp.float32) * factor
    )
    suf_scores = jnp.where(valid, suf_scores, -1e30)
    own_score = (
        jnp.einsum(
            "skgd,skd->skg",
            heads,
            key_new.reshape(stream_count, kv_local, HD),
            preferred_element_type=jnp.float32,
        )
        * factor
    )
    peak = lax.pmax(jnp.maximum(jnp.maximum(pre_peak, suf_scores.max(axis=3)), own_score), "grp")
    peak_grouped = peak[group_order].reshape(prefix_local, per_group, kv_local, groups)
    pre_weights = jnp.exp(pre_scores - peak_grouped[..., None]).astype(jnp.bfloat16)
    unit = jnp.zeros((HD,), pre_value.dtype).at[0].set(1)
    pre_value_ext = jnp.concatenate(
        [pre_value, jnp.broadcast_to(unit, pre_value.shape)], axis=3
    )
    pre_both = jnp.einsum(
        "pskgj,pjkd->pskgd", pre_weights, pre_value_ext, preferred_element_type=jnp.float32
    )
    pre_both = pre_both.reshape(stream_count, kv_local, groups, 2 * HD)[target]
    suf_weights = jnp.where(valid, jnp.exp(suf_scores - peak[:, :, :, None]), 0.0).astype(
        jnp.bfloat16
    )
    total = pre_both[..., HD] + suf_weights.astype(jnp.float32).sum(axis=3)
    numer = pre_both[..., :HD] + jnp.einsum(
        "skgj,sjkd->skgd", suf_weights, suf_value, preferred_element_type=jnp.float32
    )
    flat = stream_count, kv_local * groups
    packed = jnp.concatenate([numer.reshape(stream_count, -1), total.reshape(flat)], axis=1)
    reduced = lax.psum_scatter(packed, "grp", scatter_dimension=0, tiled=True)
    quarter = reduced.shape[0]
    q_start = lax.axis_index("grp") * quarter
    width = kv_local * groups * HD
    numer = reduced[:, :width].reshape(quarter, kv_local, groups, HD)
    total = reduced[:, width:].reshape(quarter, kv_local, groups)
    own_score = lax.dynamic_slice_in_dim(own_score, q_start, quarter, 0)
    own_peak = lax.dynamic_slice_in_dim(peak, q_start, quarter, 0)
    own_weight = jnp.exp(own_score - own_peak).astype(jnp.bfloat16).astype(jnp.float32)
    total = total + own_weight
    own_value = lax.dynamic_slice_in_dim(value_new, q_start, quarter, 0)
    own_value = own_value.reshape(quarter, kv_local, 1, HD).astype(jnp.float32)
    numer = numer + own_weight[..., None] * own_value
    attended = (numer / total[..., None]).reshape(quarter, q_local * HD).astype(jnp.bfloat16)
    attended = lax.all_gather(attended, "grp", axis=0, tiled=True)
    partial_out = jnp.dot(attended, w_out, preferred_element_type=jnp.float32)
    share = stream_count // (lax.axis_size("z") * lax.axis_size("xlo"))
    tp_start = (lax.axis_index("z") * lax.axis_size("xlo") + lax.axis_index("xlo")) * share
    summed = ring_reduce(partial_out.astype(jnp.bfloat16), "z")
    summed = pair_reduce(summed, "xlo")
    own_hidden = lax.dynamic_slice_in_dim(hidden_float, tp_start, share, 0)
    middle = (own_hidden + summed.astype(jnp.float32)).astype(jnp.bfloat16)
    middle_float = middle.astype(jnp.float32)
    ffn_squares = lax.psum(jnp.sum(middle_float * middle_float, axis=1), "grp")
    ffn_inverse = lax.rsqrt(ffn_squares / D + epsilon)
    normed_own = (middle_float * ffn_inverse[:, None] * ffn_gain).astype(jnp.bfloat16)
    swap = [(0, 1), (1, 0)]
    gate_both = jnp.concatenate([w_gate, lax.ppermute(w_gate, "core", swap)], axis=1)
    up_both = jnp.concatenate([w_up, lax.ppermute(w_up, "core", swap)], axis=1)
    down_both = jnp.concatenate([w_down, lax.ppermute(w_down, "core", swap)], axis=0)
    normed_row = pair_gather(pair_gather(normed_own, "xlo"), "hi")
    normed_half = ring_gather(normed_row, "z")
    hidden_units = gate_both.shape[1]
    part_gate = jnp.dot(normed_half, gate_both, preferred_element_type=jnp.float32)
    part_upward = jnp.dot(normed_half, up_both, preferred_element_type=jnp.float32)
    both = jnp.concatenate([part_gate, part_upward], axis=1).astype(jnp.bfloat16)
    reduced = lax.psum_scatter(both, "grp", scatter_dimension=0, tiled=True).astype(jnp.float32)
    gate = reduced[:, :hidden_units]
    upward = reduced[:, hidden_units:]
    act = (jax.nn.silu(gate) * upward).astype(jnp.bfloat16)
    act_all = lax.all_gather(act, "grp", axis=0, tiled=True)
    down = jnp.dot(act_all, down_both, preferred_element_type=jnp.float32)
    returned = ring_reduce(down.astype(jnp.bfloat16), "z").astype(jnp.bfloat16)
    returned = pair_reduce(pair_reduce(returned, "hi").astype(jnp.bfloat16), "xlo")
    return (middle_float + returned.astype(jnp.float32)).astype(jnp.bfloat16)


def solution(mesh):
    pool = ("hi", "core")
    chip_mesh = jax.sharding.Mesh(
        mesh.devices.reshape(
            mesh.shape["pool"] // 2, 2, mesh.shape["grp"], mesh.shape["tp"] // 2, 2
        ),
        ("hi", "core", "grp", "z", "xlo"),
    )
    return jax.shard_map(
        body,
        mesh=chip_mesh,
        in_specs=(
            P(pool, "grp"),
            P("grp"),
            P("grp", TP),
            P("grp", TP),
            P("grp", TP),
            P(TP, "grp"),
            P(pool, "grp", TP),
            P(pool, "grp", TP),
            P(pool, "grp", TP),
            P(pool, "grp", TP),
            P(pool),
            P(pool),
            P("grp"),
            P("grp", pool + TP),
            P("grp", pool + TP),
            P(pool + TP, "grp"),
        ),
        out_specs=P(pool + TP, "grp"),
        check_vma=False,
    )
```

```python
import math

import jax
import jax.numpy as jnp
from jax import lax
from jax.sharding import PartitionSpec as P

D = 8192
HD = 128
TP = ("z", "xlo")


epsilon = 1e-05


def joined(array, axis, combine):
    everything = jax.tree.map(lambda part: lax.all_gather(part, axis), array)
    first = jax.tree.map(lambda part: part[0], everything)

    def lap(k, so_far):
        return combine(so_far, jax.tree.map(lambda part: part[k], everything))

    return lax.fori_loop(1, lax.axis_size(axis), lap, first)


def combine_parts(earlier, later):
    peak_one, total_one, numer_one = earlier
    peak_two, total_two, numer_two = later
    peak = jnp.maximum(peak_one, peak_two)
    scale_one = jnp.exp(peak_one - peak)
    scale_two = jnp.exp(peak_two - peak)
    total = total_one * scale_one + total_two * scale_two
    numer = numer_one * scale_one[..., None] + numer_two * scale_two[..., None]
    return (peak, total, numer)


def pair_gather(part, axis):
    swap = [(0, 1), (1, 0)]
    other = lax.ppermute(part, axis, swap)
    first = lax.axis_index(axis) == 0
    return jnp.where(
        first, jnp.concatenate([part, other], axis=0), jnp.concatenate([other, part], axis=0)
    )


def pair_reduce(rows, axis):
    swap = [(0, 1), (1, 0)]
    index = lax.axis_index(axis)
    halves = rows.reshape((2, rows.shape[0] // 2) + rows.shape[1:])
    mine = lax.dynamic_index_in_dim(halves, index, 0, keepdims=False)
    other = lax.dynamic_index_in_dim(halves, 1 - index, 0, keepdims=False)
    other = lax.ppermute(other.astype(jnp.bfloat16), axis, swap)
    return mine.astype(jnp.float32) + other.astype(jnp.float32)


def ring_gather(part, axis):
    size = lax.axis_size(axis)
    index = lax.axis_index(axis)
    pieces = [part]
    for shift in range(1, size):
        pairs = [(i, (i + shift) % size) for i in range(size)]
        pieces.append(lax.ppermute(part, axis, pairs))
    stacked = jnp.stack(pieces)
    order = (index - jnp.arange(size, dtype=jnp.int32)) % size
    return stacked[order].reshape((size * part.shape[0],) + part.shape[1:])


def ring_reduce(rows, axis):
    size = lax.axis_size(axis)
    index = lax.axis_index(axis)
    blocks = rows.reshape((size, rows.shape[0] // size) + rows.shape[1:])
    total = lax.dynamic_index_in_dim(blocks, index, 0, keepdims=False).astype(jnp.float32)
    for shift in range(1, size):
        pairs = [(i, (i + shift) % size) for i in range(size)]
        outgoing = lax.dynamic_index_in_dim(blocks, (index + shift) % size, 0, keepdims=False)
        total = total + lax.ppermute(outgoing, axis, pairs).astype(jnp.float32)
    return total


def body(
    hidden,
    attn_gain,
    w_query,
    w_key,
    w_value,
    w_out,
    prefix_keys,
    prefix_values,
    suffix_keys,
    suffix_values,
    prefix_ids,
    suffix_lens,
    ffn_gain,
    w_gate,
    w_up,
    w_down,
):
    stream_count = hidden.shape[0]
    hidden_float = hidden.astype(jnp.float32)
    squares = lax.psum(jnp.sum(hidden_float * hidden_float, axis=1), "grp")
    inverse = lax.rsqrt(squares / D + epsilon)
    normed = (hidden_float * inverse[:, None] * attn_gain).astype(jnp.bfloat16)
    part_query = jnp.dot(normed, w_query, preferred_element_type=jnp.float32)
    part_key = jnp.dot(normed, w_key, preferred_element_type=jnp.float32)
    part_value = jnp.dot(normed, w_value, preferred_element_type=jnp.float32)
    query, key_new, value_new = lax.psum((part_query, part_key, part_value), "grp")
    query = query.astype(jnp.bfloat16)
    key_new = key_new.astype(jnp.bfloat16)
    value_new = value_new.astype(jnp.bfloat16)
    kv_local = w_key.shape[1] // HD
    q_local = w_query.shape[1] // HD
    groups = q_local // kv_local
    prefix_local = prefix_keys.shape[0]
    pre_length = prefix_keys.shape[1]
    suf_length = suffix_keys.shape[1]
    factor = 1.0 / math.sqrt(HD)
    heads = query.reshape(stream_count, kv_local, groups, HD)
    pre_key = prefix_keys.reshape(prefix_local, pre_length, kv_local, HD)
    pre_value = prefix_values.reshape(prefix_local, pre_length, kv_local, HD)
    suf_key = suffix_keys.reshape(stream_count, suf_length, kv_local, HD)
    suf_value = suffix_values.reshape(stream_count, suf_length, kv_local, HD)
    pool_index = lax.axis_index("hi") * lax.axis_size("core") + lax.axis_index("core")
    local_prefix = prefix_ids - pool_index * prefix_local
    per_group = stream_count // prefix_local
    one_hot = (local_prefix[:, None] == jnp.arange(prefix_local, dtype=jnp.int32)[None, :]).astype(
        jnp.int32
    )
    rank_within = jnp.sum(jnp.cumsum(one_hot, axis=0) * one_hot, axis=1) - 1
    target = local_prefix * per_group + rank_within
    group_order = (
        jnp.zeros((stream_count,), jnp.int32)
        .at[target]
        .set(jnp.arange(stream_count, dtype=jnp.int32))
    )
    grouped = heads[group_order].reshape(prefix_local, per_group, kv_local, groups, HD)
    pre_scores = (
        jnp.einsum("pskgd,pjkd->pskgj", grouped, pre_key, preferred_element_type=jnp.float32)
        * factor
    )
    pre_peak = pre_scores.max(axis=4).reshape(stream_count, kv_local, groups)[target]
    positions = lax.axis_index("grp") * suf_length + jnp.arange(suf_length, dtype=jnp.int32)
    valid = (positions[None, :] < suffix_lens[:, None])[:, None, None, :]
    suf_scores = (
        jnp.einsum("skgd,sjkd->skgj", heads, suf_key, preferred_element_type=jnp.float32) * factor
    )
    suf_scores = jnp.where(valid, suf_scores, -1e30)
    own_score = (
        jnp.einsum(
            "skgd,skd->skg",
            heads,
            key_new.reshape(stream_count, kv_local, HD),
            preferred_element_type=jnp.float32,
        )
        * factor
    )
    peak = lax.pmax(jnp.maximum(jnp.maximum(pre_peak, suf_scores.max(axis=3)), own_score), "grp")
    peak_grouped = peak[group_order].reshape(prefix_local, per_group, kv_local, groups)
    pre_weights = jnp.exp(pre_scores - peak_grouped[..., None]).astype(jnp.bfloat16)
    unit = jnp.zeros((HD,), pre_value.dtype).at[0].set(1)
    pre_value_ext = jnp.concatenate(
        [pre_value, jnp.broadcast_to(unit, pre_value.shape)], axis=3
    )
    pre_both = jnp.einsum(
        "pskgj,pjkd->pskgd", pre_weights, pre_value_ext, preferred_element_type=jnp.float32
    )
    pre_both = pre_both.reshape(stream_count, kv_local, groups, 2 * HD)[target]
    suf_weights = jnp.where(valid, jnp.exp(suf_scores - peak[:, :, :, None]), 0.0).astype(
        jnp.bfloat16
    )
    total = pre_both[..., HD] + suf_weights.astype(jnp.float32).sum(axis=3)
    numer = pre_both[..., :HD] + jnp.einsum(
        "skgj,sjkd->skgd", suf_weights, suf_value, preferred_element_type=jnp.float32
    )
    flat = stream_count, kv_local * groups
    packed = jnp.concatenate([numer.reshape(stream_count, -1), total.reshape(flat)], axis=1)
    reduced = ring_reduce(packed, "grp")
    quarter = reduced.shape[0]
    q_start = lax.axis_index("grp") * quarter
    width = kv_local * groups * HD
    numer = reduced[:, :width].reshape(quarter, kv_local, groups, HD)
    total = reduced[:, width:].reshape(quarter, kv_local, groups)
    own_score = lax.dynamic_slice_in_dim(own_score, q_start, quarter, 0)
    own_peak = lax.dynamic_slice_in_dim(peak, q_start, quarter, 0)
    own_weight = jnp.exp(own_score - own_peak).astype(jnp.bfloat16).astype(jnp.float32)
    total = total + own_weight
    own_value = lax.dynamic_slice_in_dim(value_new, q_start, quarter, 0)
    own_value = own_value.reshape(quarter, kv_local, 1, HD).astype(jnp.float32)
    numer = numer + own_weight[..., None] * own_value
    attended = (numer / total[..., None]).reshape(quarter, q_local * HD).astype(jnp.bfloat16)
    attended = ring_gather(attended, "grp")
    partial_out = jnp.dot(attended, w_out, preferred_element_type=jnp.float32)
    share = stream_count // (lax.axis_size("z") * lax.axis_size("xlo"))
    tp_start = (lax.axis_index("z") * lax.axis_size("xlo") + lax.axis_index("xlo")) * share
    summed = ring_reduce(partial_out.astype(jnp.bfloat16), "z")
    summed = pair_reduce(summed, "xlo")
    own_hidden = lax.dynamic_slice_in_dim(hidden_float, tp_start, share, 0)
    middle = (own_hidden + summed.astype(jnp.float32)).astype(jnp.bfloat16)
    middle_float = middle.astype(jnp.float32)
    ffn_squares = lax.psum(jnp.sum(middle_float * middle_float, axis=1), "grp")
    ffn_inverse = lax.rsqrt(ffn_squares / D + epsilon)
    normed_own = (middle_float * ffn_inverse[:, None] * ffn_gain).astype(jnp.bfloat16)
    swap = [(0, 1), (1, 0)]
    gate_both = jnp.concatenate([w_gate, lax.ppermute(w_gate, "core", swap)], axis=1)
    up_both = jnp.concatenate([w_up, lax.ppermute(w_up, "core", swap)], axis=1)
    down_both = jnp.concatenate([w_down, lax.ppermute(w_down, "core", swap)], axis=0)
    normed_row = pair_gather(pair_gather(normed_own, "xlo"), "hi")
    normed_half = ring_gather(normed_row, "z")
    hidden_units = gate_both.shape[1]
    part_gate = jnp.dot(normed_half, gate_both, preferred_element_type=jnp.float32)
    part_upward = jnp.dot(normed_half, up_both, preferred_element_type=jnp.float32)
    both = jnp.concatenate([part_gate, part_upward], axis=1).astype(jnp.bfloat16)
    reduced = ring_reduce(both, "grp")
    gate = reduced[:, :hidden_units]
    upward = reduced[:, hidden_units:]
    act = (jax.nn.silu(gate) * upward).astype(jnp.bfloat16)
    act_all = ring_gather(act, "grp")
    down = jnp.dot(act_all, down_both, preferred_element_type=jnp.float32)
    returned = ring_reduce(down.astype(jnp.bfloat16), "z").astype(jnp.bfloat16)
    returned = pair_reduce(pair_reduce(returned, "hi").astype(jnp.bfloat16), "xlo")
    return (middle_float + returned.astype(jnp.float32)).astype(jnp.bfloat16)


def solution(mesh):
    pool = ("hi", "core")
    chip_mesh = jax.sharding.Mesh(
        mesh.devices.reshape(
            mesh.shape["pool"] // 2, 2, mesh.shape["grp"], mesh.shape["tp"] // 2, 2
        ),
        ("hi", "core", "grp", "z", "xlo"),
    )
    return jax.shard_map(
        body,
        mesh=chip_mesh,
        in_specs=(
            P(pool, "grp"),
            P("grp"),
            P("grp", TP),
            P("grp", TP),
            P("grp", TP),
            P(TP, "grp"),
            P(pool, "grp", TP),
            P(pool, "grp", TP),
            P(pool, "grp", TP),
            P(pool, "grp", TP),
            P(pool),
            P(pool),
            P("grp"),
            P("grp", pool + TP),
            P("grp", pool + TP),
            P(pool + TP, "grp"),
        ),
        out_specs=P(pool + TP, "grp"),
        check_vma=False,
    )
```

```python
import math

import jax
import jax.numpy as jnp
from jax import lax
from jax.sharding import PartitionSpec as P

D = 8192
HD = 128
TP = ("z", "xlo")


epsilon = 1e-05


def joined(array, axis, combine):
    everything = jax.tree.map(lambda part: lax.all_gather(part, axis), array)
    first = jax.tree.map(lambda part: part[0], everything)

    def lap(k, so_far):
        return combine(so_far, jax.tree.map(lambda part: part[k], everything))

    return lax.fori_loop(1, lax.axis_size(axis), lap, first)


def combine_parts(earlier, later):
    peak_one, total_one, numer_one = earlier
    peak_two, total_two, numer_two = later
    peak = jnp.maximum(peak_one, peak_two)
    scale_one = jnp.exp(peak_one - peak)
    scale_two = jnp.exp(peak_two - peak)
    total = total_one * scale_one + total_two * scale_two
    numer = numer_one * scale_one[..., None] + numer_two * scale_two[..., None]
    return (peak, total, numer)


def pair_gather(part, axis):
    swap = [(0, 1), (1, 0)]
    other = lax.ppermute(part, axis, swap)
    first = lax.axis_index(axis) == 0
    return jnp.where(
        first, jnp.concatenate([part, other], axis=0), jnp.concatenate([other, part], axis=0)
    )


def pair_reduce(rows, axis):
    swap = [(0, 1), (1, 0)]
    index = lax.axis_index(axis)
    halves = rows.reshape((2, rows.shape[0] // 2) + rows.shape[1:])
    mine = lax.dynamic_index_in_dim(halves, index, 0, keepdims=False)
    other = lax.dynamic_index_in_dim(halves, 1 - index, 0, keepdims=False)
    other = lax.ppermute(other.astype(jnp.bfloat16), axis, swap)
    return mine.astype(jnp.float32) + other.astype(jnp.float32)


def ring_gather(part, axis):
    size = lax.axis_size(axis)
    index = lax.axis_index(axis)
    pieces = [part]
    for shift in range(1, size):
        pairs = [(i, (i + shift) % size) for i in range(size)]
        pieces.append(lax.ppermute(part, axis, pairs))
    stacked = jnp.stack(pieces)
    order = (index - jnp.arange(size, dtype=jnp.int32)) % size
    return stacked[order].reshape((size * part.shape[0],) + part.shape[1:])


def ring_reduce(rows, axis):
    size = lax.axis_size(axis)
    index = lax.axis_index(axis)
    blocks = rows.reshape((size, rows.shape[0] // size) + rows.shape[1:])
    total = lax.dynamic_index_in_dim(blocks, index, 0, keepdims=False).astype(jnp.float32)
    for shift in range(1, size):
        pairs = [(i, (i + shift) % size) for i in range(size)]
        outgoing = lax.dynamic_index_in_dim(blocks, (index + shift) % size, 0, keepdims=False)
        total = total + lax.ppermute(outgoing, axis, pairs).astype(jnp.float32)
    return total


def small_reduce(value, axis, combine):
    return combine(ring_gather(value[None], axis), axis=0)


def body(
    hidden,
    attn_gain,
    w_query,
    w_key,
    w_value,
    w_out,
    prefix_keys,
    prefix_values,
    suffix_keys,
    suffix_values,
    prefix_ids,
    suffix_lens,
    ffn_gain,
    w_gate,
    w_up,
    w_down,
):
    stream_count = hidden.shape[0]
    hidden_float = hidden.astype(jnp.float32)
    squares = small_reduce(jnp.sum(hidden_float * hidden_float, axis=1), "grp", jnp.sum)
    inverse = lax.rsqrt(squares / D + epsilon)
    normed = (hidden_float * inverse[:, None] * attn_gain).astype(jnp.bfloat16)
    part_query = jnp.dot(normed, w_query, preferred_element_type=jnp.float32)
    part_key = jnp.dot(normed, w_key, preferred_element_type=jnp.float32)
    part_value = jnp.dot(normed, w_value, preferred_element_type=jnp.float32)
    query, key_new, value_new = lax.psum((part_query, part_key, part_value), "grp")
    query = query.astype(jnp.bfloat16)
    key_new = key_new.astype(jnp.bfloat16)
    value_new = value_new.astype(jnp.bfloat16)
    kv_local = w_key.shape[1] // HD
    q_local = w_query.shape[1] // HD
    groups = q_local // kv_local
    prefix_local = prefix_keys.shape[0]
    pre_length = prefix_keys.shape[1]
    suf_length = suffix_keys.shape[1]
    factor = 1.0 / math.sqrt(HD)
    heads = query.reshape(stream_count, kv_local, groups, HD)
    pre_key = prefix_keys.reshape(prefix_local, pre_length, kv_local, HD)
    pre_value = prefix_values.reshape(prefix_local, pre_length, kv_local, HD)
    suf_key = suffix_keys.reshape(stream_count, suf_length, kv_local, HD)
    suf_value = suffix_values.reshape(stream_count, suf_length, kv_local, HD)
    pool_index = lax.axis_index("hi") * lax.axis_size("core") + lax.axis_index("core")
    local_prefix = prefix_ids - pool_index * prefix_local
    per_group = stream_count // prefix_local
    one_hot = (local_prefix[:, None] == jnp.arange(prefix_local, dtype=jnp.int32)[None, :]).astype(
        jnp.int32
    )
    rank_within = jnp.sum(jnp.cumsum(one_hot, axis=0) * one_hot, axis=1) - 1
    target = local_prefix * per_group + rank_within
    group_order = (
        jnp.zeros((stream_count,), jnp.int32)
        .at[target]
        .set(jnp.arange(stream_count, dtype=jnp.int32))
    )
    grouped = heads[group_order].reshape(prefix_local, per_group, kv_local, groups, HD)
    pre_scores = (
        jnp.einsum("pskgd,pjkd->pskgj", grouped, pre_key, preferred_element_type=jnp.float32)
        * factor
    )
    pre_peak = pre_scores.max(axis=4).reshape(stream_count, kv_local, groups)[target]
    positions = lax.axis_index("grp") * suf_length + jnp.arange(suf_length, dtype=jnp.int32)
    valid = (positions[None, :] < suffix_lens[:, None])[:, None, None, :]
    suf_scores = (
        jnp.einsum("skgd,sjkd->skgj", heads, suf_key, preferred_element_type=jnp.float32) * factor
    )
    suf_scores = jnp.where(valid, suf_scores, -1e30)
    own_score = (
        jnp.einsum(
            "skgd,skd->skg",
            heads,
            key_new.reshape(stream_count, kv_local, HD),
            preferred_element_type=jnp.float32,
        )
        * factor
    )
    peak = jnp.maximum(jnp.maximum(pre_peak, suf_scores.max(axis=3)), own_score)
    peak = small_reduce(peak, "grp", jnp.max)
    peak_grouped = peak[group_order].reshape(prefix_local, per_group, kv_local, groups)
    pre_weights = jnp.exp(pre_scores - peak_grouped[..., None]).astype(jnp.bfloat16)
    unit = jnp.zeros((HD,), pre_value.dtype).at[0].set(1)
    pre_value_ext = jnp.concatenate(
        [pre_value, jnp.broadcast_to(unit, pre_value.shape)], axis=3
    )
    pre_both = jnp.einsum(
        "pskgj,pjkd->pskgd", pre_weights, pre_value_ext, preferred_element_type=jnp.float32
    )
    pre_both = pre_both.reshape(stream_count, kv_local, groups, 2 * HD)[target]
    suf_weights = jnp.where(valid, jnp.exp(suf_scores - peak[:, :, :, None]), 0.0).astype(
        jnp.bfloat16
    )
    total = pre_both[..., HD] + suf_weights.astype(jnp.float32).sum(axis=3)
    numer = pre_both[..., :HD] + jnp.einsum(
        "skgj,sjkd->skgd", suf_weights, suf_value, preferred_element_type=jnp.float32
    )
    flat = stream_count, kv_local * groups
    packed = jnp.concatenate([numer.reshape(stream_count, -1), total.reshape(flat)], axis=1)
    reduced = ring_reduce(packed, "grp")
    quarter = reduced.shape[0]
    q_start = lax.axis_index("grp") * quarter
    width = kv_local * groups * HD
    numer = reduced[:, :width].reshape(quarter, kv_local, groups, HD)
    total = reduced[:, width:].reshape(quarter, kv_local, groups)
    own_score = lax.dynamic_slice_in_dim(own_score, q_start, quarter, 0)
    own_peak = lax.dynamic_slice_in_dim(peak, q_start, quarter, 0)
    own_weight = jnp.exp(own_score - own_peak).astype(jnp.bfloat16).astype(jnp.float32)
    total = total + own_weight
    own_value = lax.dynamic_slice_in_dim(value_new, q_start, quarter, 0)
    own_value = own_value.reshape(quarter, kv_local, 1, HD).astype(jnp.float32)
    numer = numer + own_weight[..., None] * own_value
    attended = (numer / total[..., None]).reshape(quarter, q_local * HD).astype(jnp.bfloat16)
    attended = ring_gather(attended, "grp")
    partial_out = jnp.dot(attended, w_out, preferred_element_type=jnp.float32)
    share = stream_count // (lax.axis_size("z") * lax.axis_size("xlo"))
    tp_start = (lax.axis_index("z") * lax.axis_size("xlo") + lax.axis_index("xlo")) * share
    summed = ring_reduce(partial_out.astype(jnp.bfloat16), "z")
    summed = pair_reduce(summed, "xlo")
    own_hidden = lax.dynamic_slice_in_dim(hidden_float, tp_start, share, 0)
    middle = (own_hidden + summed.astype(jnp.float32)).astype(jnp.bfloat16)
    middle_float = middle.astype(jnp.float32)
    ffn_squares = small_reduce(jnp.sum(middle_float * middle_float, axis=1), "grp", jnp.sum)
    ffn_inverse = lax.rsqrt(ffn_squares / D + epsilon)
    normed_own = (middle_float * ffn_inverse[:, None] * ffn_gain).astype(jnp.bfloat16)
    swap = [(0, 1), (1, 0)]
    gate_both = jnp.concatenate([w_gate, lax.ppermute(w_gate, "core", swap)], axis=1)
    up_both = jnp.concatenate([w_up, lax.ppermute(w_up, "core", swap)], axis=1)
    down_both = jnp.concatenate([w_down, lax.ppermute(w_down, "core", swap)], axis=0)
    normed_row = pair_gather(pair_gather(normed_own, "xlo"), "hi")
    normed_half = ring_gather(normed_row, "z")
    hidden_units = gate_both.shape[1]
    part_gate = jnp.dot(normed_half, gate_both, preferred_element_type=jnp.float32)
    part_upward = jnp.dot(normed_half, up_both, preferred_element_type=jnp.float32)
    both = jnp.concatenate([part_gate, part_upward], axis=1).astype(jnp.bfloat16)
    reduced = ring_reduce(both, "grp")
    gate = reduced[:, :hidden_units]
    upward = reduced[:, hidden_units:]
    act = (jax.nn.silu(gate) * upward).astype(jnp.bfloat16)
    act_all = ring_gather(act, "grp")
    down = jnp.dot(act_all, down_both, preferred_element_type=jnp.float32)
    returned = ring_reduce(down.astype(jnp.bfloat16), "z").astype(jnp.bfloat16)
    returned = pair_reduce(pair_reduce(returned, "hi").astype(jnp.bfloat16), "xlo")
    return (middle_float + returned.astype(jnp.float32)).astype(jnp.bfloat16)


def solution(mesh):
    pool = ("hi", "core")
    chip_mesh = jax.sharding.Mesh(
        mesh.devices.reshape(
            mesh.shape["pool"] // 2, 2, mesh.shape["grp"], mesh.shape["tp"] // 2, 2
        ),
        ("hi", "core", "grp", "z", "xlo"),
    )
    return jax.shard_map(
        body,
        mesh=chip_mesh,
        in_specs=(
            P(pool, "grp"),
            P("grp"),
            P("grp", TP),
            P("grp", TP),
            P("grp", TP),
            P(TP, "grp"),
            P(pool, "grp", TP),
            P(pool, "grp", TP),
            P(pool, "grp", TP),
            P(pool, "grp", TP),
            P(pool),
            P(pool),
            P("grp"),
            P("grp", pool + TP),
            P("grp", pool + TP),
            P(pool + TP, "grp"),
        ),
        out_specs=P(pool + TP, "grp"),
        check_vma=False,
    )
```

```python
import math

import jax
import jax.numpy as jnp
from jax import lax
from jax.sharding import PartitionSpec as P

D = 8192
HD = 128
TP = ("z", "xlo")


epsilon = 1e-05


def joined(array, axis, combine):
    everything = jax.tree.map(lambda part: lax.all_gather(part, axis), array)
    first = jax.tree.map(lambda part: part[0], everything)

    def lap(k, so_far):
        return combine(so_far, jax.tree.map(lambda part: part[k], everything))

    return lax.fori_loop(1, lax.axis_size(axis), lap, first)


def combine_parts(earlier, later):
    peak_one, total_one, numer_one = earlier
    peak_two, total_two, numer_two = later
    peak = jnp.maximum(peak_one, peak_two)
    scale_one = jnp.exp(peak_one - peak)
    scale_two = jnp.exp(peak_two - peak)
    total = total_one * scale_one + total_two * scale_two
    numer = numer_one * scale_one[..., None] + numer_two * scale_two[..., None]
    return (peak, total, numer)


def pair_gather(part, axis):
    swap = [(0, 1), (1, 0)]
    other = lax.ppermute(part, axis, swap)
    first = lax.axis_index(axis) == 0
    return jnp.where(
        first, jnp.concatenate([part, other], axis=0), jnp.concatenate([other, part], axis=0)
    )


def pair_reduce(rows, axis):
    swap = [(0, 1), (1, 0)]
    index = lax.axis_index(axis)
    halves = rows.reshape((2, rows.shape[0] // 2) + rows.shape[1:])
    mine = lax.dynamic_index_in_dim(halves, index, 0, keepdims=False)
    other = lax.dynamic_index_in_dim(halves, 1 - index, 0, keepdims=False)
    other = lax.ppermute(other.astype(jnp.bfloat16), axis, swap)
    return mine.astype(jnp.float32) + other.astype(jnp.float32)


def ring_gather(part, axis):
    size = lax.axis_size(axis)
    index = lax.axis_index(axis)
    pieces = [part]
    for shift in range(1, size):
        pairs = [(i, (i + shift) % size) for i in range(size)]
        pieces.append(lax.ppermute(part, axis, pairs))
    stacked = jnp.stack(pieces)
    order = (index - jnp.arange(size, dtype=jnp.int32)) % size
    return stacked[order].reshape((size * part.shape[0],) + part.shape[1:])


def ring_reduce(rows, axis):
    size = lax.axis_size(axis)
    index = lax.axis_index(axis)
    blocks = rows.reshape((size, rows.shape[0] // size) + rows.shape[1:])
    total = lax.dynamic_index_in_dim(blocks, index, 0, keepdims=False).astype(jnp.float32)
    for shift in range(1, size):
        pairs = [(i, (i + shift) % size) for i in range(size)]
        outgoing = lax.dynamic_index_in_dim(blocks, (index + shift) % size, 0, keepdims=False)
        total = total + lax.ppermute(outgoing, axis, pairs).astype(jnp.float32)
    return total


def small_reduce(value, axis, combine):
    return combine(ring_gather(value[None], axis), axis=0)


def body(
    hidden,
    attn_gain,
    w_query,
    w_key,
    w_value,
    w_out,
    prefix_keys,
    prefix_values,
    suffix_keys,
    suffix_values,
    prefix_ids,
    suffix_lens,
    ffn_gain,
    w_gate,
    w_up,
    w_down,
):
    stream_count = hidden.shape[0]
    hidden_float = hidden.astype(jnp.float32)
    squares = small_reduce(jnp.sum(hidden_float * hidden_float, axis=1), "grp", jnp.sum)
    inverse = lax.rsqrt(squares / D + epsilon)
    normed = (hidden_float * inverse[:, None] * attn_gain).astype(jnp.bfloat16)
    part_query = jnp.dot(normed, w_query, preferred_element_type=jnp.float32)
    part_key = jnp.dot(normed, w_key, preferred_element_type=jnp.float32)
    part_value = jnp.dot(normed, w_value, preferred_element_type=jnp.float32)
    projected = jnp.concatenate([part_query, part_key, part_value], axis=1)
    projected = ring_gather(ring_reduce(projected, "grp").astype(jnp.bfloat16), "grp")
    q_width = part_query.shape[1]
    k_width = part_key.shape[1]
    query = projected[:, :q_width]
    key_new = projected[:, q_width : q_width + k_width]
    value_new = projected[:, q_width + k_width :]
    kv_local = w_key.shape[1] // HD
    q_local = w_query.shape[1] // HD
    groups = q_local // kv_local
    prefix_local = prefix_keys.shape[0]
    pre_length = prefix_keys.shape[1]
    suf_length = suffix_keys.shape[1]
    factor = 1.0 / math.sqrt(HD)
    heads = query.reshape(stream_count, kv_local, groups, HD)
    pre_key = prefix_keys.reshape(prefix_local, pre_length, kv_local, HD)
    pre_value = prefix_values.reshape(prefix_local, pre_length, kv_local, HD)
    suf_key = suffix_keys.reshape(stream_count, suf_length, kv_local, HD)
    suf_value = suffix_values.reshape(stream_count, suf_length, kv_local, HD)
    pool_index = lax.axis_index("hi") * lax.axis_size("core") + lax.axis_index("core")
    local_prefix = prefix_ids - pool_index * prefix_local
    per_group = stream_count // prefix_local
    one_hot = (local_prefix[:, None] == jnp.arange(prefix_local, dtype=jnp.int32)[None, :]).astype(
        jnp.int32
    )
    rank_within = jnp.sum(jnp.cumsum(one_hot, axis=0) * one_hot, axis=1) - 1
    target = local_prefix * per_group + rank_within
    group_order = (
        jnp.zeros((stream_count,), jnp.int32)
        .at[target]
        .set(jnp.arange(stream_count, dtype=jnp.int32))
    )
    grouped = heads[group_order].reshape(prefix_local, per_group, kv_local, groups, HD)
    pre_scores = (
        jnp.einsum("pskgd,pjkd->pskgj", grouped, pre_key, preferred_element_type=jnp.float32)
        * factor
    )
    pre_peak = pre_scores.max(axis=4).reshape(stream_count, kv_local, groups)[target]
    positions = lax.axis_index("grp") * suf_length + jnp.arange(suf_length, dtype=jnp.int32)
    valid = (positions[None, :] < suffix_lens[:, None])[:, None, None, :]
    suf_scores = (
        jnp.einsum("skgd,sjkd->skgj", heads, suf_key, preferred_element_type=jnp.float32) * factor
    )
    suf_scores = jnp.where(valid, suf_scores, -1e30)
    own_score = (
        jnp.einsum(
            "skgd,skd->skg",
            heads,
            key_new.reshape(stream_count, kv_local, HD),
            preferred_element_type=jnp.float32,
        )
        * factor
    )
    peak = jnp.maximum(jnp.maximum(pre_peak, suf_scores.max(axis=3)), own_score)
    peak = small_reduce(peak, "grp", jnp.max)
    peak_grouped = peak[group_order].reshape(prefix_local, per_group, kv_local, groups)
    pre_weights = jnp.exp(pre_scores - peak_grouped[..., None]).astype(jnp.bfloat16)
    unit = jnp.zeros((HD,), pre_value.dtype).at[0].set(1)
    pre_value_ext = jnp.concatenate(
        [pre_value, jnp.broadcast_to(unit, pre_value.shape)], axis=3
    )
    pre_both = jnp.einsum(
        "pskgj,pjkd->pskgd", pre_weights, pre_value_ext, preferred_element_type=jnp.float32
    )
    pre_both = pre_both.reshape(stream_count, kv_local, groups, 2 * HD)[target]
    suf_weights = jnp.where(valid, jnp.exp(suf_scores - peak[:, :, :, None]), 0.0).astype(
        jnp.bfloat16
    )
    total = pre_both[..., HD] + suf_weights.astype(jnp.float32).sum(axis=3)
    numer = pre_both[..., :HD] + jnp.einsum(
        "skgj,sjkd->skgd", suf_weights, suf_value, preferred_element_type=jnp.float32
    )
    flat = stream_count, kv_local * groups
    packed = jnp.concatenate([numer.reshape(stream_count, -1), total.reshape(flat)], axis=1)
    reduced = ring_reduce(packed, "grp")
    quarter = reduced.shape[0]
    q_start = lax.axis_index("grp") * quarter
    width = kv_local * groups * HD
    numer = reduced[:, :width].reshape(quarter, kv_local, groups, HD)
    total = reduced[:, width:].reshape(quarter, kv_local, groups)
    own_score = lax.dynamic_slice_in_dim(own_score, q_start, quarter, 0)
    own_peak = lax.dynamic_slice_in_dim(peak, q_start, quarter, 0)
    own_weight = jnp.exp(own_score - own_peak).astype(jnp.bfloat16).astype(jnp.float32)
    total = total + own_weight
    own_value = lax.dynamic_slice_in_dim(value_new, q_start, quarter, 0)
    own_value = own_value.reshape(quarter, kv_local, 1, HD).astype(jnp.float32)
    numer = numer + own_weight[..., None] * own_value
    attended = (numer / total[..., None]).reshape(quarter, q_local * HD).astype(jnp.bfloat16)
    attended = ring_gather(attended, "grp")
    partial_out = jnp.dot(attended, w_out, preferred_element_type=jnp.float32)
    share = stream_count // (lax.axis_size("z") * lax.axis_size("xlo"))
    tp_start = (lax.axis_index("z") * lax.axis_size("xlo") + lax.axis_index("xlo")) * share
    summed = ring_reduce(partial_out.astype(jnp.bfloat16), "z")
    summed = pair_reduce(summed, "xlo")
    own_hidden = lax.dynamic_slice_in_dim(hidden_float, tp_start, share, 0)
    middle = (own_hidden + summed.astype(jnp.float32)).astype(jnp.bfloat16)
    middle_float = middle.astype(jnp.float32)
    ffn_squares = small_reduce(jnp.sum(middle_float * middle_float, axis=1), "grp", jnp.sum)
    ffn_inverse = lax.rsqrt(ffn_squares / D + epsilon)
    normed_own = (middle_float * ffn_inverse[:, None] * ffn_gain).astype(jnp.bfloat16)
    swap = [(0, 1), (1, 0)]
    gate_both = jnp.concatenate([w_gate, lax.ppermute(w_gate, "core", swap)], axis=1)
    up_both = jnp.concatenate([w_up, lax.ppermute(w_up, "core", swap)], axis=1)
    down_both = jnp.concatenate([w_down, lax.ppermute(w_down, "core", swap)], axis=0)
    normed_row = pair_gather(pair_gather(normed_own, "xlo"), "hi")
    normed_half = ring_gather(normed_row, "z")
    hidden_units = gate_both.shape[1]
    part_gate = jnp.dot(normed_half, gate_both, preferred_element_type=jnp.float32)
    part_upward = jnp.dot(normed_half, up_both, preferred_element_type=jnp.float32)
    both = jnp.concatenate([part_gate, part_upward], axis=1).astype(jnp.bfloat16)
    reduced = ring_reduce(both, "grp")
    gate = reduced[:, :hidden_units]
    upward = reduced[:, hidden_units:]
    act = (jax.nn.silu(gate) * upward).astype(jnp.bfloat16)
    act_all = ring_gather(act, "grp")
    down = jnp.dot(act_all, down_both, preferred_element_type=jnp.float32)
    returned = ring_reduce(down.astype(jnp.bfloat16), "z").astype(jnp.bfloat16)
    returned = pair_reduce(pair_reduce(returned, "hi").astype(jnp.bfloat16), "xlo")
    return (middle_float + returned.astype(jnp.float32)).astype(jnp.bfloat16)


def solution(mesh):
    pool = ("hi", "core")
    chip_mesh = jax.sharding.Mesh(
        mesh.devices.reshape(
            mesh.shape["pool"] // 2, 2, mesh.shape["grp"], mesh.shape["tp"] // 2, 2
        ),
        ("hi", "core", "grp", "z", "xlo"),
    )
    return jax.shard_map(
        body,
        mesh=chip_mesh,
        in_specs=(
            P(pool, "grp"),
            P("grp"),
            P("grp", TP),
            P("grp", TP),
            P("grp", TP),
            P(TP, "grp"),
            P(pool, "grp", TP),
            P(pool, "grp", TP),
            P(pool, "grp", TP),
            P(pool, "grp", TP),
            P(pool),
            P(pool),
            P("grp"),
            P("grp", pool + TP),
            P("grp", pool + TP),
            P(pool + TP, "grp"),
        ),
        out_specs=P(pool + TP, "grp"),
        check_vma=False,
    )
```

```python
import math

import jax
import jax.numpy as jnp
from jax import lax
from jax.sharding import PartitionSpec as P

D = 8192
HD = 128
TP = ("z", "xlo")


epsilon = 1e-05


def joined(array, axis, combine):
    everything = jax.tree.map(lambda part: lax.all_gather(part, axis), array)
    first = jax.tree.map(lambda part: part[0], everything)

    def lap(k, so_far):
        return combine(so_far, jax.tree.map(lambda part: part[k], everything))

    return lax.fori_loop(1, lax.axis_size(axis), lap, first)


def combine_parts(earlier, later):
    peak_one, total_one, numer_one = earlier
    peak_two, total_two, numer_two = later
    peak = jnp.maximum(peak_one, peak_two)
    scale_one = jnp.exp(peak_one - peak)
    scale_two = jnp.exp(peak_two - peak)
    total = total_one * scale_one + total_two * scale_two
    numer = numer_one * scale_one[..., None] + numer_two * scale_two[..., None]
    return (peak, total, numer)


def pair_gather(part, axis):
    swap = [(0, 1), (1, 0)]
    other = lax.ppermute(part, axis, swap)
    first = lax.axis_index(axis) == 0
    return jnp.where(
        first, jnp.concatenate([part, other], axis=0), jnp.concatenate([other, part], axis=0)
    )


def pair_reduce(rows, axis):
    swap = [(0, 1), (1, 0)]
    index = lax.axis_index(axis)
    halves = rows.reshape((2, rows.shape[0] // 2) + rows.shape[1:])
    mine = lax.dynamic_index_in_dim(halves, index, 0, keepdims=False)
    other = lax.dynamic_index_in_dim(halves, 1 - index, 0, keepdims=False)
    other = lax.ppermute(other.astype(jnp.bfloat16), axis, swap)
    return mine.astype(jnp.float32) + other.astype(jnp.float32)


def ring_gather(part, axis):
    size = lax.axis_size(axis)
    index = lax.axis_index(axis)
    pieces = [part]
    for shift in range(1, size):
        pairs = [(i, (i + shift) % size) for i in range(size)]
        pieces.append(lax.ppermute(part, axis, pairs))
    stacked = jnp.stack(pieces)
    order = (index - jnp.arange(size, dtype=jnp.int32)) % size
    return stacked[order].reshape((size * part.shape[0],) + part.shape[1:])


def ring_reduce(rows, axis):
    size = lax.axis_size(axis)
    index = lax.axis_index(axis)
    blocks = rows.reshape((size, rows.shape[0] // size) + rows.shape[1:])
    total = lax.dynamic_index_in_dim(blocks, index, 0, keepdims=False).astype(jnp.float32)
    for shift in range(1, size):
        pairs = [(i, (i + shift) % size) for i in range(size)]
        outgoing = lax.dynamic_index_in_dim(blocks, (index + shift) % size, 0, keepdims=False)
        total = total + lax.ppermute(outgoing, axis, pairs).astype(jnp.float32)
    return total


def small_reduce(value, axis, combine):
    return combine(ring_gather(value[None], axis), axis=0)


def body(
    hidden,
    attn_gain,
    w_query,
    w_key,
    w_value,
    w_out,
    prefix_keys,
    prefix_values,
    suffix_keys,
    suffix_values,
    prefix_ids,
    suffix_lens,
    ffn_gain,
    w_gate,
    w_up,
    w_down,
):
    stream_count = hidden.shape[0]
    hidden_float = hidden.astype(jnp.float32)
    squares = small_reduce(jnp.sum(hidden_float * hidden_float, axis=1), "grp", jnp.sum)
    inverse = lax.rsqrt(squares / D + epsilon)
    normed = (hidden_float * inverse[:, None] * attn_gain).astype(jnp.bfloat16)
    part_query = jnp.dot(normed, w_query, preferred_element_type=jnp.float32)
    part_key = jnp.dot(normed, w_key, preferred_element_type=jnp.float32)
    part_value = jnp.dot(normed, w_value, preferred_element_type=jnp.float32)
    projected = jnp.concatenate([part_query, part_key, part_value], axis=1)
    projected = ring_gather(ring_reduce(projected, "grp").astype(jnp.bfloat16), "grp")
    q_width = part_query.shape[1]
    k_width = part_key.shape[1]
    query = projected[:, :q_width]
    key_new = projected[:, q_width : q_width + k_width]
    value_new = projected[:, q_width + k_width :]
    kv_local = w_key.shape[1] // HD
    q_local = w_query.shape[1] // HD
    groups = q_local // kv_local
    prefix_local = prefix_keys.shape[0]
    pre_length = prefix_keys.shape[1]
    suf_length = suffix_keys.shape[1]
    factor = 1.0 / math.sqrt(HD)
    heads = query.reshape(stream_count, kv_local, groups, HD)
    pre_key = prefix_keys.reshape(prefix_local, pre_length, kv_local, HD)
    pre_value = prefix_values.reshape(prefix_local, pre_length, kv_local, HD)
    suf_key = suffix_keys.reshape(stream_count, suf_length, kv_local, HD)
    suf_value = suffix_values.reshape(stream_count, suf_length, kv_local, HD)
    pool_index = lax.axis_index("hi") * lax.axis_size("core") + lax.axis_index("core")
    local_prefix = prefix_ids - pool_index * prefix_local
    per_group = stream_count // prefix_local
    one_hot = (local_prefix[:, None] == jnp.arange(prefix_local, dtype=jnp.int32)[None, :]).astype(
        jnp.int32
    )
    rank_within = jnp.sum(jnp.cumsum(one_hot, axis=0) * one_hot, axis=1) - 1
    target = local_prefix * per_group + rank_within
    group_order = (
        jnp.zeros((stream_count,), jnp.int32)
        .at[target]
        .set(jnp.arange(stream_count, dtype=jnp.int32))
    )
    grouped = heads[group_order].reshape(prefix_local, per_group, kv_local, groups, HD)
    pre_scores = (
        jnp.einsum("pskgd,pjkd->pskgj", grouped, pre_key, preferred_element_type=jnp.float32)
        * factor
    )
    pre_peak = pre_scores.max(axis=4).reshape(stream_count, kv_local, groups)[target]
    positions = lax.axis_index("grp") * suf_length + jnp.arange(suf_length, dtype=jnp.int32)
    valid = (positions[None, :] < suffix_lens[:, None])[:, None, None, :]
    suf_scores = (
        jnp.einsum("skgd,sjkd->skgj", heads, suf_key, preferred_element_type=jnp.float32) * factor
    )
    suf_scores = jnp.where(valid, suf_scores, -1e30)
    own_score = (
        jnp.einsum(
            "skgd,skd->skg",
            heads,
            key_new.reshape(stream_count, kv_local, HD),
            preferred_element_type=jnp.float32,
        )
        * factor
    )
    peak = jnp.maximum(jnp.maximum(pre_peak, suf_scores.max(axis=3)), own_score)
    peak = small_reduce(peak, "grp", jnp.max)
    peak_grouped = peak[group_order].reshape(prefix_local, per_group, kv_local, groups)
    pre_weights = jnp.exp(pre_scores - peak_grouped[..., None]).astype(jnp.bfloat16)
    unit = jnp.zeros((HD,), pre_value.dtype).at[0].set(1)
    pre_value_ext = jnp.concatenate(
        [pre_value, jnp.broadcast_to(unit, pre_value.shape)], axis=3
    )
    pre_both = jnp.einsum(
        "pskgj,pjkd->pskgd", pre_weights, pre_value_ext, preferred_element_type=jnp.float32
    )
    pre_both = pre_both.reshape(stream_count, kv_local, groups, 2 * HD)[target]
    suf_weights = jnp.where(valid, jnp.exp(suf_scores - peak[:, :, :, None]), 0.0).astype(
        jnp.bfloat16
    )
    total = pre_both[..., HD] + suf_weights.astype(jnp.float32).sum(axis=3)
    numer = pre_both[..., :HD] + jnp.einsum(
        "skgj,sjkd->skgd", suf_weights, suf_value, preferred_element_type=jnp.float32
    )
    flat = stream_count, kv_local * groups
    packed = jnp.concatenate([numer.reshape(stream_count, -1), total.reshape(flat)], axis=1)
    reduced = ring_reduce(packed, "grp")
    quarter = reduced.shape[0]
    q_start = lax.axis_index("grp") * quarter
    width = kv_local * groups * HD
    numer = reduced[:, :width].reshape(quarter, kv_local, groups, HD)
    total = reduced[:, width:].reshape(quarter, kv_local, groups)
    own_score = lax.dynamic_slice_in_dim(own_score, q_start, quarter, 0)
    own_peak = lax.dynamic_slice_in_dim(peak, q_start, quarter, 0)
    own_weight = jnp.exp(own_score - own_peak).astype(jnp.bfloat16).astype(jnp.float32)
    total = total + own_weight
    own_value = lax.dynamic_slice_in_dim(value_new, q_start, quarter, 0)
    own_value = own_value.reshape(quarter, kv_local, 1, HD).astype(jnp.float32)
    numer = numer + own_weight[..., None] * own_value
    attended = (numer / total[..., None]).reshape(quarter, q_local * HD).astype(jnp.bfloat16)
    attended = ring_gather(attended, "grp")
    partial_out = jnp.dot(attended, w_out, preferred_element_type=jnp.float32)
    share = stream_count // (lax.axis_size("z") * lax.axis_size("xlo"))
    tp_start = (lax.axis_index("z") * lax.axis_size("xlo") + lax.axis_index("xlo")) * share
    summed = ring_reduce(partial_out.astype(jnp.bfloat16), "z")
    summed = pair_reduce(summed, "xlo")
    own_hidden = lax.dynamic_slice_in_dim(hidden_float, tp_start, share, 0)
    middle = (own_hidden + summed.astype(jnp.float32)).astype(jnp.bfloat16)
    middle_float = middle.astype(jnp.float32)
    ffn_squares = small_reduce(jnp.sum(middle_float * middle_float, axis=1), "grp", jnp.sum)
    ffn_inverse = lax.rsqrt(ffn_squares / D + epsilon)
    normed_own = (middle_float * ffn_inverse[:, None] * ffn_gain).astype(jnp.bfloat16)
    swap = [(0, 1), (1, 0)]
    other_gate = lax.ppermute(w_gate, "core", swap)
    other_up = lax.ppermute(w_up, "core", swap)
    other_down = lax.ppermute(w_down, "core", swap)
    normed_row = pair_gather(pair_gather(normed_own, "xlo"), "hi")
    normed_half = ring_gather(normed_row, "z")
    hidden_units = 2 * w_gate.shape[1]
    pieces = [
        jnp.dot(normed_half, weight, preferred_element_type=jnp.float32)
        for weight in (w_gate, other_gate, w_up, other_up)
    ]
    both = jnp.concatenate(pieces, axis=1).astype(jnp.bfloat16)
    reduced = ring_reduce(both, "grp")
    gate = reduced[:, :hidden_units]
    upward = reduced[:, hidden_units:]
    act = (jax.nn.silu(gate) * upward).astype(jnp.bfloat16)
    act_all = ring_gather(act, "grp")
    own_units = w_down.shape[0]
    down = jnp.dot(act_all[:, :own_units], w_down, preferred_element_type=jnp.float32)
    down = down + jnp.dot(act_all[:, own_units:], other_down, preferred_element_type=jnp.float32)
    returned = ring_reduce(down.astype(jnp.bfloat16), "z").astype(jnp.bfloat16)
    returned = pair_reduce(pair_reduce(returned, "hi").astype(jnp.bfloat16), "xlo")
    return (middle_float + returned.astype(jnp.float32)).astype(jnp.bfloat16)


def solution(mesh):
    pool = ("hi", "core")
    chip_mesh = jax.sharding.Mesh(
        mesh.devices.reshape(
            mesh.shape["pool"] // 2, 2, mesh.shape["grp"], mesh.shape["tp"] // 2, 2
        ),
        ("hi", "core", "grp", "z", "xlo"),
    )
    return jax.shard_map(
        body,
        mesh=chip_mesh,
        in_specs=(
            P(pool, "grp"),
            P("grp"),
            P("grp", TP),
            P("grp", TP),
            P("grp", TP),
            P(TP, "grp"),
            P(pool, "grp", TP),
            P(pool, "grp", TP),
            P(pool, "grp", TP),
            P(pool, "grp", TP),
            P(pool),
            P(pool),
            P("grp"),
            P("grp", pool + TP),
            P("grp", pool + TP),
            P(pool + TP, "grp"),
        ),
        out_specs=P(pool + TP, "grp"),
        check_vma=False,
    )
```

```python
import math

import jax
import jax.numpy as jnp
from jax import lax
from jax.sharding import PartitionSpec as P

D = 8192
HD = 128
TP = ("z", "xlo")


epsilon = 1e-05


def joined(array, axis, combine):
    everything = jax.tree.map(lambda part: lax.all_gather(part, axis), array)
    first = jax.tree.map(lambda part: part[0], everything)

    def lap(k, so_far):
        return combine(so_far, jax.tree.map(lambda part: part[k], everything))

    return lax.fori_loop(1, lax.axis_size(axis), lap, first)


def combine_parts(earlier, later):
    peak_one, total_one, numer_one = earlier
    peak_two, total_two, numer_two = later
    peak = jnp.maximum(peak_one, peak_two)
    scale_one = jnp.exp(peak_one - peak)
    scale_two = jnp.exp(peak_two - peak)
    total = total_one * scale_one + total_two * scale_two
    numer = numer_one * scale_one[..., None] + numer_two * scale_two[..., None]
    return (peak, total, numer)


def pair_gather(part, axis):
    swap = [(0, 1), (1, 0)]
    other = lax.ppermute(part, axis, swap)
    first = lax.axis_index(axis) == 0
    return jnp.where(
        first, jnp.concatenate([part, other], axis=0), jnp.concatenate([other, part], axis=0)
    )


def pair_reduce(rows, axis):
    swap = [(0, 1), (1, 0)]
    index = lax.axis_index(axis)
    halves = rows.reshape((2, rows.shape[0] // 2) + rows.shape[1:])
    mine = lax.dynamic_index_in_dim(halves, index, 0, keepdims=False)
    other = lax.dynamic_index_in_dim(halves, 1 - index, 0, keepdims=False)
    other = lax.ppermute(other.astype(jnp.bfloat16), axis, swap)
    return mine.astype(jnp.float32) + other.astype(jnp.float32)


def ring_gather(part, axis):
    size = lax.axis_size(axis)
    index = lax.axis_index(axis)
    pieces = [part]
    for shift in range(1, size):
        pairs = [(i, (i + shift) % size) for i in range(size)]
        pieces.append(lax.ppermute(part, axis, pairs))
    stacked = jnp.stack(pieces)
    order = (index - jnp.arange(size, dtype=jnp.int32)) % size
    return stacked[order].reshape((size * part.shape[0],) + part.shape[1:])


def ring_reduce(rows, axis):
    size = lax.axis_size(axis)
    index = lax.axis_index(axis)
    blocks = rows.reshape((size, rows.shape[0] // size) + rows.shape[1:])
    total = lax.dynamic_index_in_dim(blocks, index, 0, keepdims=False).astype(jnp.float32)
    for shift in range(1, size):
        pairs = [(i, (i + shift) % size) for i in range(size)]
        outgoing = lax.dynamic_index_in_dim(blocks, (index + shift) % size, 0, keepdims=False)
        total = total + lax.ppermute(outgoing, axis, pairs).astype(jnp.float32)
    return total


def ring_gather_relative(part, axis):
    size = lax.axis_size(axis)
    pieces = [part]
    for shift in range(1, size):
        pairs = [(i, (i + shift) % size) for i in range(size)]
        pieces.append(lax.ppermute(part, axis, pairs))
    return jnp.concatenate(pieces, axis=0)


def ring_reduce_relative(rows, axis):
    size = lax.axis_size(axis)
    blocks = rows.reshape((size, rows.shape[0] // size) + rows.shape[1:])
    total = blocks[0].astype(jnp.float32)
    for shift in range(1, size):
        pairs = [(i, (i + shift) % size) for i in range(size)]
        outgoing = blocks[(size - shift) % size]
        total = total + lax.ppermute(outgoing, axis, pairs).astype(jnp.float32)
    return total


def small_reduce(value, axis, combine):
    return combine(ring_gather(value[None], axis), axis=0)


def body(
    hidden,
    attn_gain,
    w_query,
    w_key,
    w_value,
    w_out,
    prefix_keys,
    prefix_values,
    suffix_keys,
    suffix_values,
    prefix_ids,
    suffix_lens,
    ffn_gain,
    w_gate,
    w_up,
    w_down,
):
    stream_count = hidden.shape[0]
    hidden_float = hidden.astype(jnp.float32)
    squares = small_reduce(jnp.sum(hidden_float * hidden_float, axis=1), "grp", jnp.sum)
    inverse = lax.rsqrt(squares / D + epsilon)
    normed = (hidden_float * inverse[:, None] * attn_gain).astype(jnp.bfloat16)
    part_query = jnp.dot(normed, w_query, preferred_element_type=jnp.float32)
    part_key = jnp.dot(normed, w_key, preferred_element_type=jnp.float32)
    part_value = jnp.dot(normed, w_value, preferred_element_type=jnp.float32)
    projected = jnp.concatenate([part_query, part_key, part_value], axis=1)
    projected = ring_gather(ring_reduce(projected, "grp").astype(jnp.bfloat16), "grp")
    q_width = part_query.shape[1]
    k_width = part_key.shape[1]
    query = projected[:, :q_width]
    key_new = projected[:, q_width : q_width + k_width]
    value_new = projected[:, q_width + k_width :]
    kv_local = w_key.shape[1] // HD
    q_local = w_query.shape[1] // HD
    groups = q_local // kv_local
    prefix_local = prefix_keys.shape[0]
    pre_length = prefix_keys.shape[1]
    suf_length = suffix_keys.shape[1]
    factor = 1.0 / math.sqrt(HD)
    heads = query.reshape(stream_count, kv_local, groups, HD)
    pre_key = prefix_keys.reshape(prefix_local, pre_length, kv_local, HD)
    pre_value = prefix_values.reshape(prefix_local, pre_length, kv_local, HD)
    suf_key = suffix_keys.reshape(stream_count, suf_length, kv_local, HD)
    suf_value = suffix_values.reshape(stream_count, suf_length, kv_local, HD)
    pool_index = lax.axis_index("hi") * lax.axis_size("core") + lax.axis_index("core")
    local_prefix = prefix_ids - pool_index * prefix_local
    per_group = stream_count // prefix_local
    one_hot = (local_prefix[:, None] == jnp.arange(prefix_local, dtype=jnp.int32)[None, :]).astype(
        jnp.int32
    )
    rank_within = jnp.sum(jnp.cumsum(one_hot, axis=0) * one_hot, axis=1) - 1
    target = local_prefix * per_group + rank_within
    group_order = (
        jnp.zeros((stream_count,), jnp.int32)
        .at[target]
        .set(jnp.arange(stream_count, dtype=jnp.int32))
    )
    grouped = heads[group_order].reshape(prefix_local, per_group, kv_local, groups, HD)
    pre_scores = (
        jnp.einsum("pskgd,pjkd->pskgj", grouped, pre_key, preferred_element_type=jnp.float32)
        * factor
    )
    pre_peak = pre_scores.max(axis=4).reshape(stream_count, kv_local, groups)[target]
    positions = lax.axis_index("grp") * suf_length + jnp.arange(suf_length, dtype=jnp.int32)
    valid = (positions[None, :] < suffix_lens[:, None])[:, None, None, :]
    suf_scores = (
        jnp.einsum("skgd,sjkd->skgj", heads, suf_key, preferred_element_type=jnp.float32) * factor
    )
    suf_scores = jnp.where(valid, suf_scores, -1e30)
    own_score = (
        jnp.einsum(
            "skgd,skd->skg",
            heads,
            key_new.reshape(stream_count, kv_local, HD),
            preferred_element_type=jnp.float32,
        )
        * factor
    )
    peak = jnp.maximum(jnp.maximum(pre_peak, suf_scores.max(axis=3)), own_score)
    peak = small_reduce(peak, "grp", jnp.max)
    peak_grouped = peak[group_order].reshape(prefix_local, per_group, kv_local, groups)
    pre_weights = jnp.exp(pre_scores - peak_grouped[..., None]).astype(jnp.bfloat16)
    unit = jnp.zeros((HD,), pre_value.dtype).at[0].set(1)
    pre_value_ext = jnp.concatenate(
        [pre_value, jnp.broadcast_to(unit, pre_value.shape)], axis=3
    )
    pre_both = jnp.einsum(
        "pskgj,pjkd->pskgd", pre_weights, pre_value_ext, preferred_element_type=jnp.float32
    )
    pre_both = pre_both.reshape(stream_count, kv_local, groups, 2 * HD)[target]
    suf_weights = jnp.where(valid, jnp.exp(suf_scores - peak[:, :, :, None]), 0.0).astype(
        jnp.bfloat16
    )
    total = pre_both[..., HD] + suf_weights.astype(jnp.float32).sum(axis=3)
    numer = pre_both[..., :HD] + jnp.einsum(
        "skgj,sjkd->skgd", suf_weights, suf_value, preferred_element_type=jnp.float32
    )
    flat = stream_count, kv_local * groups
    packed = jnp.concatenate([numer.reshape(stream_count, -1), total.reshape(flat)], axis=1)
    reduced = ring_reduce(packed, "grp")
    quarter = reduced.shape[0]
    q_start = lax.axis_index("grp") * quarter
    width = kv_local * groups * HD
    numer = reduced[:, :width].reshape(quarter, kv_local, groups, HD)
    total = reduced[:, width:].reshape(quarter, kv_local, groups)
    own_score = lax.dynamic_slice_in_dim(own_score, q_start, quarter, 0)
    own_peak = lax.dynamic_slice_in_dim(peak, q_start, quarter, 0)
    own_weight = jnp.exp(own_score - own_peak).astype(jnp.bfloat16).astype(jnp.float32)
    total = total + own_weight
    own_value = lax.dynamic_slice_in_dim(value_new, q_start, quarter, 0)
    own_value = own_value.reshape(quarter, kv_local, 1, HD).astype(jnp.float32)
    numer = numer + own_weight[..., None] * own_value
    attended = (numer / total[..., None]).reshape(quarter, q_local * HD).astype(jnp.bfloat16)
    attended = ring_gather(attended, "grp")
    partial_out = jnp.dot(attended, w_out, preferred_element_type=jnp.float32)
    share = stream_count // (lax.axis_size("z") * lax.axis_size("xlo"))
    tp_start = (lax.axis_index("z") * lax.axis_size("xlo") + lax.axis_index("xlo")) * share
    summed = ring_reduce(partial_out.astype(jnp.bfloat16), "z")
    summed = pair_reduce(summed, "xlo")
    own_hidden = lax.dynamic_slice_in_dim(hidden_float, tp_start, share, 0)
    middle = (own_hidden + summed.astype(jnp.float32)).astype(jnp.bfloat16)
    middle_float = middle.astype(jnp.float32)
    ffn_squares = small_reduce(jnp.sum(middle_float * middle_float, axis=1), "grp", jnp.sum)
    ffn_inverse = lax.rsqrt(ffn_squares / D + epsilon)
    normed_own = (middle_float * ffn_inverse[:, None] * ffn_gain).astype(jnp.bfloat16)
    swap = [(0, 1), (1, 0)]
    gate_both = jnp.concatenate([w_gate, lax.ppermute(w_gate, "core", swap)], axis=1)
    up_both = jnp.concatenate([w_up, lax.ppermute(w_up, "core", swap)], axis=1)
    down_both = jnp.concatenate([w_down, lax.ppermute(w_down, "core", swap)], axis=0)
    normed_row = pair_gather(pair_gather(normed_own, "xlo"), "hi")
    normed_half = ring_gather_relative(normed_row, "z")
    hidden_units = gate_both.shape[1]
    part_gate = jnp.dot(normed_half, gate_both, preferred_element_type=jnp.float32)
    part_upward = jnp.dot(normed_half, up_both, preferred_element_type=jnp.float32)
    both = jnp.concatenate([part_gate, part_upward], axis=1).astype(jnp.bfloat16)
    reduced = ring_reduce(both, "grp")
    gate = reduced[:, :hidden_units]
    upward = reduced[:, hidden_units:]
    act = (jax.nn.silu(gate) * upward).astype(jnp.bfloat16)
    act_all = ring_gather(act, "grp")
    down = jnp.dot(act_all, down_both, preferred_element_type=jnp.float32)
    returned = ring_reduce_relative(down.astype(jnp.bfloat16), "z").astype(jnp.bfloat16)
    returned = pair_reduce(pair_reduce(returned, "hi").astype(jnp.bfloat16), "xlo")
    return (middle_float + returned.astype(jnp.float32)).astype(jnp.bfloat16)


def solution(mesh):
    pool = ("hi", "core")
    chip_mesh = jax.sharding.Mesh(
        mesh.devices.reshape(
            mesh.shape["pool"] // 2, 2, mesh.shape["grp"], mesh.shape["tp"] // 2, 2
        ),
        ("hi", "core", "grp", "z", "xlo"),
    )
    return jax.shard_map(
        body,
        mesh=chip_mesh,
        in_specs=(
            P(pool, "grp"),
            P("grp"),
            P("grp", TP),
            P("grp", TP),
            P("grp", TP),
            P(TP, "grp"),
            P(pool, "grp", TP),
            P(pool, "grp", TP),
            P(pool, "grp", TP),
            P(pool, "grp", TP),
            P(pool),
            P(pool),
            P("grp"),
            P("grp", pool + TP),
            P("grp", pool + TP),
            P(pool + TP, "grp"),
        ),
        out_specs=P(pool + TP, "grp"),
        check_vma=False,
    )
```
